32 devices in a mesh: row: 8 (over y, x, core), grp: 4 (over z).
Axes of the slice: x: 2, y: 2, z: 4, core: 2. Of those that a mesh axis runs over, the one named last changes fastest.
Arguments:
- basis: bfloat16 [2, 96, 24576], P(None, None, ('grp', 'row'))
- body_infl: bfloat16 [24576, 24576], P('grp', 'row'), may hold values from -0.0390625 to 0.0390625
- wake_columns: bfloat16 [64, 64, 24576], P(('row', 'grp')), may hold values from -0.023925781 to 0.023925781
- residual: float32 [2, 24576], P(None, ('row', 'grp')), may hold values from -6 to 6
- te_panels: int32 [2, 32], replicated, may hold values from 0 to 24575, as said below
- slot_strip: int32 [64], replicated, may hold values from -1 to 31, as said below
- freq_index: int32 [1], replicated, may hold values from 0 to 47
Outputs:
- q_basis: float32 [2, 96, 24576], P(None, None, ('row', 'grp'))
- new_basis: float32 [2, 96, 24576], P(None, None, ('grp', 'row'))
- coeffs: float32 [96], replicated
- new_residual: float32 [2, 24576], P(None, ('row', 'grp'))
The draws below stay inside these ranges and needn't reach their ends.
Inputs may be any that keep to these rules, and one draw needn't show every extreme that they name: `te_panels`: every panel index is different; both 0 and 24575 occur. `slot_strip`: slots s * 2 to s * 2 + 1 belong to device s of row+grp; every strip 0 to 31 is held in exactly one slot; a device holds 0 to 2 strips and some device holds 2.
All inputs are finite; a program needn't handle non-finite values.
Results may differ from the reference program's by a relative error of at most 0.00065.
Values may be sent and summed in bfloat16 or wider, within the bound.
No kernel may reach another device: no remote copies, remote signals or barrier semaphores. Data moves between devices by JAX's collectives and lax.ppermute only.
A program may use at most 128 MiB of HBM per device.

```python
import math
import jax
import jax.numpy as jnp
from jax import lax

N = 24576
K = 96
P_SIZE = 64
NFREQ = 48
NS = 32
SLOTS = 64
N_GRP = 4


def draw_basis(key, part):
    key_values, key_rows, key_columns = jax.random.split(key, 3)
    position = jnp.arange(N, dtype=jnp.float32) / N
    values = jax.random.normal(key_values, (2, K, N), jnp.float32)
    row_scale = 10.0 ** jax.random.uniform(key_rows, (1, K, 1), jnp.float32)
    column_scale = (3.0 ** position)[None, None, :] * 10.0 ** jax.random.uniform(key_columns, (1, 1, N), jnp.float32)
    return (values * row_scale * column_scale).astype(jnp.bfloat16)


def draw_te_panels(key, part):
    chosen = jax.random.permutation(jax.random.fold_in(key, 11), N)[:2 * NS].astype(jnp.int32)
    chosen = jnp.where(chosen == jnp.min(chosen), 0, chosen)
    chosen = jnp.where(chosen == jnp.max(chosen), N - 1, chosen)
    return chosen.reshape(2, NS).astype(jnp.int32)


def draw_slot_strip(key, part):
    key_pairs, key_kinds, key_picks, key_strips = jax.random.split(jax.random.fold_in(key, 23), 4)
    order = jax.random.permutation(key_pairs, NS)
    kinds = jax.random.randint(key_kinds, (NS // 2,), 0, 3).at[0].set(0)
    first_count = jnp.where(kinds == 0, 2, jnp.where(kinds == 1, 0, 1)).astype(jnp.int32)
    pair_counts = jnp.stack([first_count, 2 - first_count], axis=1).reshape(-1)
    counts = jnp.zeros((NS,), jnp.int32).at[order].set(pair_counts)
    picks = jax.random.randint(key_picks, (NS,), 0, 2)
    slot_zero = (counts == 2) | (counts == 1) & (picks == 0)
    slot_one = (counts == 2) | (counts == 1) & (picks == 1)
    filled = jnp.stack([slot_zero, slot_one], axis=1).reshape(-1)
    ranks = jnp.cumsum(filled.astype(jnp.int32)) - 1
    strips = jax.random.permutation(key_strips, NS).astype(jnp.int32)
    return jnp.where(filled, strips[jnp.clip(ranks, 0, NS - 1)], -1).astype(jnp.int32)


def block_levels(stream_key, shape, cuts, smallest, top_value):
    gain, own = 1.0, jax.random.fold_in(stream_key, 6)
    for dim, parts in cuts:
        heights = jnp.exp(jax.random.uniform(jax.random.fold_in(own, dim), (parts,), jnp.float32, smallest / len(cuts), top_value / len(cuts)))
        gain = gain * jnp.repeat(heights, shape[dim] // parts).reshape([-1 if axis == dim else 1 for axis in range(len(shape))])
    return gain


def gaussian(key, shape, scale, reach, shards=(), kind=jnp.bfloat16):
    values = jax.random.normal(key, shape, jnp.float32) * scale
    if len(shards) > 0:
        values = block_levels(key, shape, shards, -0.22, 0.18) * values
    return jnp.clip(values, min=-reach, max=reach).astype(kind)


def setup_inputs(seed: int = 0) -> dict:
    seeds = jax.random.split(jax.random.key(seed), 8)
    return {
        "basis": draw_basis(jax.random.fold_in(seeds[7], 71), 0),
        "body_infl": gaussian(seeds[1], (N, N), N ** -0.5, 0.0390625, ((0, 4), (1, 8))),
        "wake_columns": gaussian(seeds[2], (SLOTS, P_SIZE, N), 0.004, 0.023925781, ((0, 32),)),
        "residual": gaussian(seeds[3], (2, N), 1.0, 6.0, ((1, 32),), jnp.float32),
        "te_panels": draw_te_panels(jax.random.fold_in(seeds[7], 71), 0),
        "slot_strip": draw_slot_strip(jax.random.fold_in(seeds[7], 71), 0),
        "freq_index": jax.random.randint(seeds[6], (1,), 0, NFREQ).astype(jnp.int32),
    }


def phase_table(freq_index, panel_count):
    wavenumber = (freq_index[0].astype(jnp.float32) + 1.0) * 0.0625
    angles = (jnp.arange(panel_count, dtype=jnp.float32) + 0.5) * 0.5 * wavenumber
    return jnp.stack([jnp.cos(angles), -jnp.sin(angles)]).astype(jnp.bfloat16)

def wake_left(strength, vectors):
    real_part = strength[:vectors]
    imag_part = strength[vectors:]
    top = jnp.concatenate([real_part, -imag_part], axis=1)
    bottom = jnp.concatenate([imag_part, real_part], axis=1)
    return jnp.concatenate([top, bottom], axis=0)

def solve_rows(factor, values):
    vectors = values.shape[1]
    width = values.shape[2]
    stacked = values.transpose(1, 0, 2).reshape(vectors, 2 * width)
    solved = lax.linalg.triangular_solve(factor, stacked, left_side=True, lower=True)
    return solved.reshape(vectors, 2, width).transpose(1, 0, 2)

def reference(basis, body_infl, wake_columns, residual, te_panels, slot_strip, freq_index):
    phases = phase_table(freq_index, P_SIZE)

    def phase_slot(columns):
        return jnp.dot(phases.astype(jnp.float32), columns.astype(jnp.float32), preferred_element_type=jnp.float32).astype(jnp.bfloat16)
    wake_phased = lax.map(phase_slot, wake_columns)
    filled = slot_strip >= 0
    strip_ids = jnp.maximum(slot_strip, 0)
    upper_panel = te_panels[0][strip_ids]
    lower_panel = te_panels[1][strip_ids]
    basis_wide = basis.astype(jnp.float32)
    difference = basis_wide[:, :, upper_panel] - basis_wide[:, :, lower_panel]
    strength = jnp.where(filled[None, None, :], difference, 0.0).astype(jnp.bfloat16)
    basis_rows = basis.reshape(2 * K, N)
    block = N // N_GRP

    def add_block(block_index, totals):
        first_index = (block_index * block).astype(jnp.int32)
        sources = lax.dynamic_slice_in_dim(basis_rows, first_index, block, 1)
        influence = lax.dynamic_slice_in_dim(body_infl, first_index, block, 0)
        return totals + jnp.dot(sources.astype(jnp.float32), influence.astype(jnp.float32), preferred_element_type=jnp.float32)
    body_part = lax.fori_loop(0, N_GRP, add_block, jnp.zeros((2 * K, N), jnp.float32))
    left_side = wake_left(strength.reshape(2 * K, SLOTS), K)
    right_side = wake_phased.transpose(1, 0, 2).reshape(2 * SLOTS, N)
    wake_part = jnp.dot(left_side.astype(jnp.float32), right_side.astype(jnp.float32), preferred_element_type=jnp.float32)
    image_rows = (body_part + wake_part).reshape(2, K, N)
    gram_matrix = jnp.einsum('akt,alt->kl', image_rows, image_rows, precision=lax.Precision.HIGHEST) / (2.0 * N)
    factor = jnp.linalg.cholesky(gram_matrix)
    q_basis = solve_rows(factor, image_rows)
    new_basis = solve_rows(factor, basis_wide)
    root_count = math.sqrt(2.0 * N)
    coeffs = jnp.einsum('akt,at->k', q_basis, residual, precision=lax.Precision.HIGHEST) / root_count
    new_residual = residual - jnp.einsum('k,akt->at', coeffs, q_basis, precision=lax.Precision.HIGHEST) / root_count
    return (q_basis, new_basis, coeffs, new_residual)
```

```python
import math

import jax
import jax.numpy as jnp
from jax import lax
from jax.sharding import PartitionSpec as P


def phase_table(freq_index, panel_count):
    wavenumber = (freq_index[0].astype(jnp.float32) + 1.0) * 0.0625
    angles = (jnp.arange(panel_count, dtype=jnp.float32) + 0.5) * 0.5 * wavenumber
    return jnp.stack([jnp.cos(angles), -jnp.sin(angles)]).astype(jnp.bfloat16)


def solve_rows(factor, values):
    vectors = values.shape[1]
    width = values.shape[2]
    stacked = values.transpose(1, 0, 2).reshape(vectors, 2 * width)
    solved = lax.linalg.triangular_solve(factor, stacked, left_side=True, lower=True)
    return solved.reshape(vectors, 2, width).transpose(1, 0, 2)


def local(basis, body_infl, wake_columns, residual, te_panels, slot_strip, freq_index):
    n_row = lax.axis_size("row")
    n_grp = lax.axis_size("grp")
    n_dev = n_row * n_grp
    vectors = basis.shape[1]
    stacked_rows = 2 * vectors
    own_cols = basis.shape[2]
    total = own_cols * n_dev
    basis_rows = basis.reshape(stacked_rows, own_cols)
    group_cols = body_infl.shape[0]
    slot_count = slot_strip.shape[0]
    local_slots = wake_columns.shape[0]
    p_size = wake_columns.shape[1]

    shard_piece = lax.all_gather(basis_rows, "row", axis=1, tiled=True)
    partial_sums = jnp.dot(shard_piece, body_infl, preferred_element_type=jnp.float32)

    filled = slot_strip >= 0
    strip_ids = jnp.maximum(slot_strip, 0)
    upper_panel = jnp.where(filled, te_panels[0][strip_ids], -1)
    lower_panel = jnp.where(filled, te_panels[1][strip_ids], -1)
    group_base = lax.axis_index("grp") * group_cols
    panels = group_base + jnp.arange(group_cols, dtype=jnp.int32)
    upper_hits = (panels[:, None] == upper_panel[None, :]).astype(jnp.float32)
    lower_hits = (panels[:, None] == lower_panel[None, :]).astype(jnp.float32)
    select = (upper_hits - lower_hits).astype(jnp.bfloat16)
    strength_own = jnp.dot(shard_piece, select, preferred_element_type=jnp.float32)
    strength_total = strength_own
    for shift in range(1, n_grp):
        perm = [(i, (i + shift) % n_grp) for i in range(n_grp)]
        strength_total = strength_total + lax.ppermute(strength_own, "grp", perm)
    strength = strength_total.astype(jnp.bfloat16)

    phases = phase_table(freq_index, p_size)
    eye = jnp.eye(local_slots, dtype=jnp.bfloat16)
    block_phases = (eye[:, None, :, None] * phases[None, :, None, :]).reshape(
        local_slots * 2, local_slots * p_size
    )
    wake_flat = wake_columns.reshape(local_slots * p_size, total)
    phased = jnp.dot(block_phases, wake_flat, preferred_element_type=jnp.float32)
    phased = phased.astype(jnp.bfloat16).reshape(local_slots * 2, n_dev, own_cols)
    outgoing = phased.transpose(1, 0, 2)
    arrived = lax.all_to_all(outgoing, ("row", "grp"), 0, 0, tiled=True)
    wake_right = arrived.reshape(slot_count * 2, own_cols)

    image_part = lax.psum_scatter(partial_sums, "grp", scatter_dimension=1, tiled=True)

    real_part = strength[:vectors]
    imag_part = strength[vectors:]
    top = jnp.stack([real_part, -imag_part], axis=2).reshape(vectors, 2 * slot_count)
    bottom = jnp.stack([imag_part, real_part], axis=2).reshape(vectors, 2 * slot_count)
    wake_left = jnp.concatenate([top, bottom], axis=0)
    wake_part = jnp.dot(wake_left, wake_right, preferred_element_type=jnp.float32)
    image_rows = (image_part + wake_part).reshape(2, vectors, own_cols)

    local_gram = jnp.einsum("akt,alt->kl", image_rows, image_rows, precision=lax.Precision.HIGHEST)
    local_proj = jnp.einsum("akt,at->k", image_rows, residual, precision=lax.Precision.HIGHEST)
    reduced = lax.psum(jnp.concatenate([local_gram, local_proj[:, None]], axis=1), ("row", "grp"))
    root_count = math.sqrt(2.0 * total)
    gram_matrix = reduced[:, :vectors] / (2.0 * total)
    factor = jnp.linalg.cholesky(gram_matrix)
    q_basis = solve_rows(factor, image_rows)
    new_basis = solve_rows(factor, basis.astype(jnp.float32))
    coeffs = lax.linalg.triangular_solve(
        factor, reduced[:, vectors:], left_side=True, lower=True
    )[:, 0] / root_count
    new_residual = (
        residual
        - jnp.einsum("k,akt->at", coeffs, q_basis, precision=lax.Precision.HIGHEST) / root_count
    )
    return (q_basis, new_basis, coeffs, new_residual)


def solution(mesh):
    in_specs = (
        P(None, None, ("grp", "row")),
        P("grp", "row"),
        P(("row", "grp"), None, None),
        P(None, ("row", "grp")),
        P(),
        P(),
        P(),
    )
    out_specs = (
        P(None, None, ("row", "grp")),
        P(None, None, ("grp", "row")),
        P(),
        P(None, ("row", "grp")),
    )
    return jax.shard_map(local, mesh=mesh, in_specs=in_specs, out_specs=out_specs, check_vma=False)
```

```python
import math

import jax
import jax.numpy as jnp
from jax import lax
from jax.sharding import PartitionSpec as P


def phase_table(freq_index, panel_count):
    wavenumber = (freq_index[0].astype(jnp.float32) + 1.0) * 0.0625
    angles = (jnp.arange(panel_count, dtype=jnp.float32) + 0.5) * 0.5 * wavenumber
    return jnp.stack([jnp.cos(angles), -jnp.sin(angles)]).astype(jnp.bfloat16)


def solve_rows(factor, values):
    vectors = values.shape[1]
    width = values.shape[2]
    stacked = values.transpose(1, 0, 2).reshape(vectors, 2 * width)
    solved = lax.linalg.triangular_solve(factor, stacked, left_side=True, lower=True)
    return solved.reshape(vectors, 2, width).transpose(1, 0, 2)


def butterfly_sum(values, axis, count):
    stride = 1
    while stride < count:
        perm = [(i, i ^ stride) for i in range(count)]
        values = values + lax.ppermute(values, axis, perm)
        stride *= 2
    return values


def local(basis, body_infl, wake_columns, residual, te_panels, slot_strip, freq_index):
    n_row = lax.axis_size("row")
    n_grp = lax.axis_size("grp")
    n_dev = n_row * n_grp
    vectors = basis.shape[1]
    stacked_rows = 2 * vectors
    own_cols = basis.shape[2]
    total = own_cols * n_dev
    basis_rows = basis.reshape(stacked_rows, own_cols)
    group_cols = body_infl.shape[0]
    slot_count = slot_strip.shape[0]
    local_slots = wake_columns.shape[0]
    p_size = wake_columns.shape[1]

    shard_piece = lax.all_gather(basis_rows, "row", axis=1, tiled=True)
    partial_sums = jnp.dot(shard_piece, body_infl, preferred_element_type=jnp.float32)

    filled = slot_strip >= 0
    strip_ids = jnp.maximum(slot_strip, 0)
    upper_panel = jnp.where(filled, te_panels[0][strip_ids], -1)
    lower_panel = jnp.where(filled, te_panels[1][strip_ids], -1)
    group_base = lax.axis_index("grp") * group_cols
    panels = group_base + jnp.arange(group_cols, dtype=jnp.int32)
    upper_hits = (panels[:, None] == upper_panel[None, :]).astype(jnp.float32)
    lower_hits = (panels[:, None] == lower_panel[None, :]).astype(jnp.float32)
    select = (upper_hits - lower_hits).astype(jnp.bfloat16)
    strength_own = jnp.dot(shard_piece, select, preferred_element_type=jnp.float32)
    strength_total = strength_own
    for shift in range(1, n_grp):
        perm = [(i, (i + shift) % n_grp) for i in range(n_grp)]
        strength_total = strength_total + lax.ppermute(strength_own, "grp", perm)
    strength = strength_total.astype(jnp.bfloat16)

    phases = phase_table(freq_index, p_size)
    eye = jnp.eye(local_slots, dtype=jnp.bfloat16)
    block_phases = (eye[:, None, :, None] * phases[None, :, None, :]).reshape(
        local_slots * 2, local_slots * p_size
    )
    wake_flat = wake_columns.reshape(local_slots * p_size, total)
    phased = jnp.dot(block_phases, wake_flat, preferred_element_type=jnp.float32)
    phased = phased.astype(jnp.bfloat16).reshape(local_slots * 2, n_dev, own_cols)
    outgoing = phased.transpose(1, 0, 2)
    arrived = lax.all_to_all(outgoing, ("row", "grp"), 0, 0, tiled=True)
    wake_right = arrived.reshape(slot_count * 2, own_cols)

    image_part = lax.psum_scatter(partial_sums, "grp", scatter_dimension=1, tiled=True)

    real_part = strength[:vectors]
    imag_part = strength[vectors:]
    top = jnp.stack([real_part, -imag_part], axis=2).reshape(vectors, 2 * slot_count)
    bottom = jnp.stack([imag_part, real_part], axis=2).reshape(vectors, 2 * slot_count)
    wake_left = jnp.concatenate([top, bottom], axis=0)
    wake_part = jnp.dot(wake_left, wake_right, preferred_element_type=jnp.float32)
    image_rows = (image_part + wake_part).reshape(2, vectors, own_cols)

    local_gram = jnp.einsum("akt,alt->kl", image_rows, image_rows, precision=lax.Precision.HIGHEST)
    local_proj = jnp.einsum("akt,at->k", image_rows, residual, precision=lax.Precision.HIGHEST)
    reduced = butterfly_sum(
        butterfly_sum(jnp.concatenate([local_gram, local_proj[:, None]], axis=1), "row", n_row),
        "grp",
        n_grp,
    )
    root_count = math.sqrt(2.0 * total)
    gram_matrix = reduced[:, :vectors] / (2.0 * total)
    factor = jnp.linalg.cholesky(gram_matrix)
    q_basis = solve_rows(factor, image_rows)
    new_basis = solve_rows(factor, basis.astype(jnp.float32))
    coeffs = lax.linalg.triangular_solve(
        factor, reduced[:, vectors:], left_side=True, lower=True
    )[:, 0] / root_count
    new_residual = (
        residual
        - jnp.einsum("k,akt->at", coeffs, q_basis, precision=lax.Precision.HIGHEST) / root_count
    )
    return (q_basis, new_basis, coeffs, new_residual)


def solution(mesh):
    in_specs = (
        P(None, None, ("grp", "row")),
        P("grp", "row"),
        P(("row", "grp"), None, None),
        P(None, ("row", "grp")),
        P(),
        P(),
        P(),
    )
    out_specs = (
        P(None, None, ("row", "grp")),
        P(None, None, ("grp", "row")),
        P(),
        P(None, ("row", "grp")),
    )
    return jax.shard_map(local, mesh=mesh, in_specs=in_specs, out_specs=out_specs, check_vma=False)
```

```python
import math

import jax
import jax.numpy as jnp
from jax import lax
from jax.sharding import PartitionSpec as P


def phase_table(freq_index, panel_count):
    wavenumber = (freq_index[0].astype(jnp.float32) + 1.0) * 0.0625
    angles = (jnp.arange(panel_count, dtype=jnp.float32) + 0.5) * 0.5 * wavenumber
    return jnp.stack([jnp.cos(angles), -jnp.sin(angles)]).astype(jnp.bfloat16)


def solve_rows(factor, values):
    vectors = values.shape[1]
    width = values.shape[2]
    stacked = values.transpose(1, 0, 2).reshape(vectors, 2 * width)
    solved = lax.linalg.triangular_solve(factor, stacked, left_side=True, lower=True)
    return solved.reshape(vectors, 2, width).transpose(1, 0, 2)


def butterfly_sum(values, axis, count):
    stride = 1
    while stride < count:
        perm = [(i, i ^ stride) for i in range(count)]
        values = values + lax.ppermute(values, axis, perm)
        stride *= 2
    return values


def local(basis, body_infl, wake_columns, residual, te_panels, slot_strip, freq_index):
    n_row = lax.axis_size("row")
    n_grp = lax.axis_size("grp")
    n_dev = n_row * n_grp
    vectors = basis.shape[1]
    stacked_rows = 2 * vectors
    own_cols = basis.shape[2]
    total = own_cols * n_dev
    basis_rows = basis.reshape(stacked_rows, own_cols)
    group_cols = body_infl.shape[0]
    slot_count = slot_strip.shape[0]
    local_slots = wake_columns.shape[0]
    p_size = wake_columns.shape[1]

    row_index = lax.axis_index("row")
    pieces = {0: basis_rows}
    for stride in range(2, n_row, 2):
        perm = [(i, i ^ stride) for i in range(n_row)]
        pieces[stride] = lax.ppermute(basis_rows, "row", perm)
    near = sorted(pieces)
    bundle = jnp.stack([pieces[k] for k in near])
    partner = lax.ppermute(bundle, "row", [(i, i ^ 1) for i in range(n_row)])
    for j, k in enumerate(near):
        pieces[k ^ 1] = partner[j]

    def source_rows(offset):
        return lax.dynamic_slice_in_dim(body_infl, (row_index ^ offset) * own_cols, own_cols, 0)

    partial_sums = None
    for k in near + [k ^ 1 for k in near]:
        term = jnp.dot(pieces[k], source_rows(k), preferred_element_type=jnp.float32)
        partial_sums = term if partial_sums is None else partial_sums + term

    filled = slot_strip >= 0
    strip_ids = jnp.maximum(slot_strip, 0)
    upper_panel = jnp.where(filled, te_panels[0][strip_ids], -1)
    lower_panel = jnp.where(filled, te_panels[1][strip_ids], -1)
    group_base = lax.axis_index("grp") * group_cols
    strength_own = None
    for k in near + [k ^ 1 for k in near]:
        first = group_base + (row_index ^ k) * own_cols
        panels = first + jnp.arange(own_cols, dtype=jnp.int32)
        upper_hits = (panels[:, None] == upper_panel[None, :]).astype(jnp.float32)
        lower_hits = (panels[:, None] == lower_panel[None, :]).astype(jnp.float32)
        select = (upper_hits - lower_hits).astype(jnp.bfloat16)
        term = jnp.dot(pieces[k], select, preferred_element_type=jnp.float32)
        strength_own = term if strength_own is None else strength_own + term
    strength_total = strength_own
    for shift in range(1, n_grp):
        perm = [(i, (i + shift) % n_grp) for i in range(n_grp)]
        strength_total = strength_total + lax.ppermute(strength_own, "grp", perm)
    strength = strength_total.astype(jnp.bfloat16)

    phases = phase_table(freq_index, p_size)
    eye = jnp.eye(local_slots, dtype=jnp.bfloat16)
    block_phases = (eye[:, None, :, None] * phases[None, :, None, :]).reshape(
        local_slots * 2, local_slots * p_size
    )
    wake_flat = wake_columns.reshape(local_slots * p_size, total)
    phased = jnp.dot(block_phases, wake_flat, preferred_element_type=jnp.float32)
    phased = phased.astype(jnp.bfloat16).reshape(local_slots * 2, n_dev, own_cols)
    outgoing = phased.transpose(1, 0, 2)
    arrived = lax.all_to_all(outgoing, ("row", "grp"), 0, 0, tiled=True)
    wake_right = arrived.reshape(slot_count * 2, own_cols)

    image_part = lax.psum_scatter(partial_sums, "grp", scatter_dimension=1, tiled=True)

    real_part = strength[:vectors]
    imag_part = strength[vectors:]
    top = jnp.stack([real_part, -imag_part], axis=2).reshape(vectors, 2 * slot_count)
    bottom = jnp.stack([imag_part, real_part], axis=2).reshape(vectors, 2 * slot_count)
    wake_left = jnp.concatenate([top, bottom], axis=0)
    wake_part = jnp.dot(wake_left, wake_right, preferred_element_type=jnp.float32)
    image_rows = (image_part + wake_part).reshape(2, vectors, own_cols)

    local_gram = jnp.einsum("akt,alt->kl", image_rows, image_rows, precision=lax.Precision.HIGHEST)
    local_proj = jnp.einsum("akt,at->k", image_rows, residual, precision=lax.Precision.HIGHEST)
    reduced = butterfly_sum(
        butterfly_sum(jnp.concatenate([local_gram, local_proj[:, None]], axis=1), "row", n_row),
        "grp",
        n_grp,
    )
    root_count = math.sqrt(2.0 * total)
    gram_matrix = reduced[:, :vectors] / (2.0 * total)
    factor = jnp.linalg.cholesky(gram_matrix)
    q_basis = solve_rows(factor, image_rows)
    new_basis = solve_rows(factor, basis.astype(jnp.float32))
    coeffs = lax.linalg.triangular_solve(
        factor, reduced[:, vectors:], left_side=True, lower=True
    )[:, 0] / root_count
    new_residual = (
        residual
        - jnp.einsum("k,akt->at", coeffs, q_basis, precision=lax.Precision.HIGHEST) / root_count
    )
    return (q_basis, new_basis, coeffs, new_residual)


def solution(mesh):
    in_specs = (
        P(None, None, ("grp", "row")),
        P("grp", "row"),
        P(("row", "grp"), None, None),
        P(None, ("row", "grp")),
        P(),
        P(),
        P(),
    )
    out_specs = (
        P(None, None, ("row", "grp")),
        P(None, None, ("grp", "row")),
        P(),
        P(None, ("row", "grp")),
    )
    return jax.shard_map(local, mesh=mesh, in_specs=in_specs, out_specs=out_specs, check_vma=False)
```

```python
import math

import jax
import jax.numpy as jnp
from jax import lax
from jax.sharding import PartitionSpec as P


def phase_table(freq_index, panel_count):
    wavenumber = (freq_index[0].astype(jnp.float32) + 1.0) * 0.0625
    angles = (jnp.arange(panel_count, dtype=jnp.float32) + 0.5) * 0.5 * wavenumber
    return jnp.stack([jnp.cos(angles), -jnp.sin(angles)]).astype(jnp.bfloat16)


def solve_rows(factor, values):
    vectors = values.shape[1]
    width = values.shape[2]
    stacked = values.transpose(1, 0, 2).reshape(vectors, 2 * width)
    solved = lax.linalg.triangular_solve(factor, stacked, left_side=True, lower=True)
    return solved.reshape(vectors, 2, width).transpose(1, 0, 2)


def butterfly_sum(values, axis, count):
    stride = 1
    while stride < count:
        perm = [(i, i ^ stride) for i in range(count)]
        values = values + lax.ppermute(values, axis, perm)
        stride *= 2
    return values


def local(basis, body_infl, wake_columns, residual, te_panels, slot_strip, freq_index):
    n_row = lax.axis_size("row")
    n_grp = lax.axis_size("grp")
    n_dev = n_row * n_grp
    vectors = basis.shape[1]
    stacked_rows = 2 * vectors
    own_cols = basis.shape[2]
    total = own_cols * n_dev
    basis_rows = basis.reshape(stacked_rows, own_cols)
    group_cols = body_infl.shape[0]
    slot_count = slot_strip.shape[0]
    local_slots = wake_columns.shape[0]
    p_size = wake_columns.shape[1]

    row_index = lax.axis_index("row")
    half = n_row // 2
    high = row_index // 2
    parity = row_index % 2
    pieces = [basis_rows]
    for stride in range(2, n_row, 2):
        perm = [(i, i ^ stride) for i in range(n_row)]
        pieces.append(lax.ppermute(basis_rows, "row", perm))
    near = jnp.stack(pieces)[jnp.arange(half, dtype=jnp.int32) ^ high]
    far = lax.ppermute(near, "row", [(i, i ^ 1) for i in range(n_row)])
    blocks = body_infl.reshape(half, 2, own_cols, body_infl.shape[1])
    near_rows = lax.dynamic_index_in_dim(blocks, parity, 1, keepdims=False)
    far_rows = lax.dynamic_index_in_dim(blocks, 1 - parity, 1, keepdims=False)
    near_sums = jnp.einsum("jkp,jpt->kt", near, near_rows, preferred_element_type=jnp.float32)
    near_sums, far = lax.optimization_barrier((near_sums, far))
    partial_sums = near_sums + jnp.einsum(
        "jkp,jpt->kt", far, far_rows, preferred_element_type=jnp.float32
    )

    filled = slot_strip >= 0
    strip_ids = jnp.maximum(slot_strip, 0)
    upper_panel = jnp.where(filled, te_panels[0][strip_ids], -1)
    lower_panel = jnp.where(filled, te_panels[1][strip_ids], -1)
    group_base = lax.axis_index("grp") * group_cols

    def select_for(side):
        first = group_base + (2 * jnp.arange(half, dtype=jnp.int32) + side) * own_cols
        panels = first[:, None] + jnp.arange(own_cols, dtype=jnp.int32)[None, :]
        upper_hits = (panels[:, :, None] == upper_panel).astype(jnp.float32)
        lower_hits = (panels[:, :, None] == lower_panel).astype(jnp.float32)
        return (upper_hits - lower_hits).astype(jnp.bfloat16)

    strength_own = jnp.einsum(
        "jkp,jps->ks", near, select_for(parity), preferred_element_type=jnp.float32
    ) + jnp.einsum("jkp,jps->ks", far, select_for(1 - parity), preferred_element_type=jnp.float32)
    strength_total = strength_own
    for shift in range(1, n_grp):
        perm = [(i, (i + shift) % n_grp) for i in range(n_grp)]
        strength_total = strength_total + lax.ppermute(strength_own, "grp", perm)
    strength = strength_total.astype(jnp.bfloat16)

    phases = phase_table(freq_index, p_size)
    eye = jnp.eye(local_slots, dtype=jnp.bfloat16)
    block_phases = (eye[:, None, :, None] * phases[None, :, None, :]).reshape(
        local_slots * 2, local_slots * p_size
    )
    wake_flat = wake_columns.reshape(local_slots * p_size, total)
    phased = jnp.dot(block_phases, wake_flat, preferred_element_type=jnp.float32)
    phased = phased.astype(jnp.bfloat16).reshape(local_slots * 2, n_dev, own_cols)
    outgoing = phased.transpose(1, 0, 2)
    arrived = lax.all_to_all(outgoing, ("row", "grp"), 0, 0, tiled=True)
    wake_right = arrived.reshape(slot_count * 2, own_cols)

    image_part = lax.psum_scatter(partial_sums, "grp", scatter_dimension=1, tiled=True)

    real_part = strength[:vectors]
    imag_part = strength[vectors:]
    top = jnp.stack([real_part, -imag_part], axis=2).reshape(vectors, 2 * slot_count)
    bottom = jnp.stack([imag_part, real_part], axis=2).reshape(vectors, 2 * slot_count)
    wake_left = jnp.concatenate([top, bottom], axis=0)
    wake_part = jnp.dot(wake_left, wake_right, preferred_element_type=jnp.float32)
    image_rows = (image_part + wake_part).reshape(2, vectors, own_cols)

    local_gram = jnp.einsum("akt,alt->kl", image_rows, image_rows, precision=lax.Precision.HIGHEST)
    local_proj = jnp.einsum("akt,at->k", image_rows, residual, precision=lax.Precision.HIGHEST)
    reduced = butterfly_sum(
        butterfly_sum(jnp.concatenate([local_gram, local_proj[:, None]], axis=1), "row", n_row),
        "grp",
        n_grp,
    )
    root_count = math.sqrt(2.0 * total)
    gram_matrix = reduced[:, :vectors] / (2.0 * total)
    factor = jnp.linalg.cholesky(gram_matrix)
    q_basis = solve_rows(factor, image_rows)
    new_basis = solve_rows(factor, basis.astype(jnp.float32))
    coeffs = lax.linalg.triangular_solve(
        factor, reduced[:, vectors:], left_side=True, lower=True
    )[:, 0] / root_count
    new_residual = (
        residual
        - jnp.einsum("k,akt->at", coeffs, q_basis, precision=lax.Precision.HIGHEST) / root_count
    )
    return (q_basis, new_basis, coeffs, new_residual)


def solution(mesh):
    in_specs = (
        P(None, None, ("grp", "row")),
        P("grp", "row"),
        P(("row", "grp"), None, None),
        P(None, ("row", "grp")),
        P(),
        P(),
        P(),
    )
    out_specs = (
        P(None, None, ("row", "grp")),
        P(None, None, ("grp", "row")),
        P(),
        P(None, ("row", "grp")),
    )
    return jax.shard_map(local, mesh=mesh, in_specs=in_specs, out_specs=out_specs, check_vma=False)
```

```python
import math

import jax
import jax.numpy as jnp
from jax import lax
from jax.sharding import PartitionSpec as P


def phase_table(freq_index, panel_count):
    wavenumber = (freq_index[0].astype(jnp.float32) + 1.0) * 0.0625
    angles = (jnp.arange(panel_count, dtype=jnp.float32) + 0.5) * 0.5 * wavenumber
    return jnp.stack([jnp.cos(angles), -jnp.sin(angles)]).astype(jnp.bfloat16)


def solve_rows(factor, values):
    vectors = values.shape[1]
    width = values.shape[2]
    stacked = values.transpose(1, 0, 2).reshape(vectors, 2 * width)
    solved = lax.linalg.triangular_solve(factor, stacked, left_side=True, lower=True)
    return solved.reshape(vectors, 2, width).transpose(1, 0, 2)


def butterfly_sum(values, axis, count):
    stride = 1
    while stride < count:
        perm = [(i, i ^ stride) for i in range(count)]
        values = values + lax.ppermute(values, axis, perm)
        stride *= 2
    return values


def local(basis, body_infl, wake_columns, residual, te_panels, slot_strip, freq_index):
    n_row = lax.axis_size("row")
    n_grp = lax.axis_size("grp")
    n_dev = n_row * n_grp
    vectors = basis.shape[1]
    stacked_rows = 2 * vectors
    own_cols = basis.shape[2]
    total = own_cols * n_dev
    basis_rows = basis.reshape(stacked_rows, own_cols)
    group_cols = body_infl.shape[0]
    slot_count = slot_strip.shape[0]
    local_slots = wake_columns.shape[0]
    p_size = wake_columns.shape[1]

    row_index = lax.axis_index("row")
    half = n_row // 2
    high = row_index // 2
    parity = row_index % 2
    pieces = [basis_rows]
    for stride in range(2, n_row, 2):
        perm = [(i, i ^ stride) for i in range(n_row)]
        pieces.append(lax.ppermute(basis_rows, "row", perm))
    near = jnp.stack(pieces)[jnp.arange(half, dtype=jnp.int32) ^ high]
    far = lax.ppermute(near, "row", [(i, i ^ 1) for i in range(n_row)])
    blocks = body_infl.reshape(half, 2, own_cols, body_infl.shape[1])
    near_rows = lax.dynamic_index_in_dim(blocks, parity, 1, keepdims=False)
    far_rows = lax.dynamic_index_in_dim(blocks, 1 - parity, 1, keepdims=False)
    grp_index = lax.axis_index("grp")
    width = body_infl.shape[1] // n_grp

    def block_product(pieces_stack, rows, block):
        cols = lax.dynamic_slice_in_dim(rows, block * width, width, axis=2)
        return jnp.einsum("jkp,jpt->kt", pieces_stack, cols, preferred_element_type=jnp.float32)

    order = list(range(1, n_grp)) + [0]
    near_sums = [block_product(near, near_rows, grp_index ^ d) for d in order]
    near_sums, far = lax.optimization_barrier((near_sums, far))
    image_part = None
    for d, near_sum in zip(order, near_sums):
        block_sum = near_sum + block_product(far, far_rows, grp_index ^ d)
        if d:
            block_sum = lax.ppermute(block_sum, "grp", [(i, i ^ d) for i in range(n_grp)])
        image_part = block_sum if image_part is None else image_part + block_sum

    filled = slot_strip >= 0
    strip_ids = jnp.maximum(slot_strip, 0)
    upper_panel = jnp.where(filled, te_panels[0][strip_ids], -1)
    lower_panel = jnp.where(filled, te_panels[1][strip_ids], -1)
    group_base = lax.axis_index("grp") * group_cols

    def select_for(side):
        first = group_base + (2 * jnp.arange(half, dtype=jnp.int32) + side) * own_cols
        panels = first[:, None] + jnp.arange(own_cols, dtype=jnp.int32)[None, :]
        upper_hits = (panels[:, :, None] == upper_panel).astype(jnp.float32)
        lower_hits = (panels[:, :, None] == lower_panel).astype(jnp.float32)
        return (upper_hits - lower_hits).astype(jnp.bfloat16)

    strength_own = jnp.einsum(
        "jkp,jps->ks", near, select_for(parity), preferred_element_type=jnp.float32
    ) + jnp.einsum("jkp,jps->ks", far, select_for(1 - parity), preferred_element_type=jnp.float32)
    strength_total = strength_own
    for shift in range(1, n_grp):
        perm = [(i, (i + shift) % n_grp) for i in range(n_grp)]
        strength_total = strength_total + lax.ppermute(strength_own, "grp", perm)
    strength = strength_total.astype(jnp.bfloat16)

    phases = phase_table(freq_index, p_size)
    eye = jnp.eye(local_slots, dtype=jnp.bfloat16)
    block_phases = (eye[:, None, :, None] * phases[None, :, None, :]).reshape(
        local_slots * 2, local_slots * p_size
    )
    wake_flat = wake_columns.reshape(local_slots * p_size, total)
    phased = jnp.dot(block_phases, wake_flat, preferred_element_type=jnp.float32)
    phased = phased.astype(jnp.bfloat16).reshape(local_slots * 2, n_dev, own_cols)
    outgoing = phased.transpose(1, 0, 2)
    arrived = lax.all_to_all(outgoing, ("row", "grp"), 0, 0, tiled=True)
    wake_right = arrived.reshape(slot_count * 2, own_cols)


    real_part = strength[:vectors]
    imag_part = strength[vectors:]
    top = jnp.stack([real_part, -imag_part], axis=2).reshape(vectors, 2 * slot_count)
    bottom = jnp.stack([imag_part, real_part], axis=2).reshape(vectors, 2 * slot_count)
    wake_left = jnp.concatenate([top, bottom], axis=0)
    wake_part = jnp.dot(wake_left, wake_right, preferred_element_type=jnp.float32)
    image_rows = (image_part + wake_part).reshape(2, vectors, own_cols)

    local_gram = jnp.einsum("akt,alt->kl", image_rows, image_rows, precision=lax.Precision.HIGHEST)
    local_proj = jnp.einsum("akt,at->k", image_rows, residual, precision=lax.Precision.HIGHEST)
    reduced = butterfly_sum(
        butterfly_sum(jnp.concatenate([local_gram, local_proj[:, None]], axis=1), "row", n_row),
        "grp",
        n_grp,
    )
    root_count = math.sqrt(2.0 * total)
    gram_matrix = reduced[:, :vectors] / (2.0 * total)
    factor = jnp.linalg.cholesky(gram_matrix)
    q_basis = solve_rows(factor, image_rows)
    new_basis = solve_rows(factor, basis.astype(jnp.float32))
    coeffs = lax.linalg.triangular_solve(
        factor, reduced[:, vectors:], left_side=True, lower=True
    )[:, 0] / root_count
    new_residual = (
        residual
        - jnp.einsum("k,akt->at", coeffs, q_basis, precision=lax.Precision.HIGHEST) / root_count
    )
    return (q_basis, new_basis, coeffs, new_residual)


def solution(mesh):
    in_specs = (
        P(None, None, ("grp", "row")),
        P("grp", "row"),
        P(("row", "grp"), None, None),
        P(None, ("row", "grp")),
        P(),
        P(),
        P(),
    )
    out_specs = (
        P(None, None, ("row", "grp")),
        P(None, None, ("grp", "row")),
        P(),
        P(None, ("row", "grp")),
    )
    return jax.shard_map(local, mesh=mesh, in_specs=in_specs, out_specs=out_specs, check_vma=False)
```

```python
import math

import jax
import jax.numpy as jnp
from jax import lax
from jax.sharding import PartitionSpec as P


def phase_table(freq_index, panel_count):
    wavenumber = (freq_index[0].astype(jnp.float32) + 1.0) * 0.0625
    angles = (jnp.arange(panel_count, dtype=jnp.float32) + 0.5) * 0.5 * wavenumber
    return jnp.stack([jnp.cos(angles), -jnp.sin(angles)]).astype(jnp.bfloat16)


def solve_rows(factor, values):
    vectors = values.shape[1]
    width = values.shape[2]
    stacked = values.transpose(1, 0, 2).reshape(vectors, 2 * width)
    solved = lax.linalg.triangular_solve(factor, stacked, left_side=True, lower=True)
    return solved.reshape(vectors, 2, width).transpose(1, 0, 2)


def butterfly_sum(values, axis, count):
    stride = 1
    while stride < count:
        perm = [(i, i ^ stride) for i in range(count)]
        values = values + lax.ppermute(values, axis, perm)
        stride *= 2
    return values


def local(basis, body_infl, wake_columns, residual, te_panels, slot_strip, freq_index):
    n_row = lax.axis_size("row")
    n_grp = lax.axis_size("grp")
    n_dev = n_row * n_grp
    vectors = basis.shape[1]
    stacked_rows = 2 * vectors
    own_cols = basis.shape[2]
    total = own_cols * n_dev
    basis_rows = basis.reshape(stacked_rows, own_cols)
    group_cols = body_infl.shape[0]
    slot_count = slot_strip.shape[0]
    local_slots = wake_columns.shape[0]
    p_size = wake_columns.shape[1]

    row_index = lax.axis_index("row")
    half = n_row // 2
    high = row_index // 2
    parity = row_index % 2
    pieces = [basis_rows]
    for stride in range(2, n_row, 2):
        perm = [(i, i ^ stride) for i in range(n_row)]
        pieces.append(lax.ppermute(basis_rows, "row", perm))
    near = jnp.stack(pieces)[jnp.arange(half, dtype=jnp.int32) ^ high]
    far = lax.ppermute(near, "row", [(i, i ^ 1) for i in range(n_row)])
    blocks = body_infl.reshape(half, 2, own_cols, body_infl.shape[1])
    near_rows = lax.dynamic_index_in_dim(blocks, parity, 1, keepdims=False)
    far_rows = lax.dynamic_index_in_dim(blocks, 1 - parity, 1, keepdims=False)
    near_sums = jnp.einsum("jkp,jpt->kt", near, near_rows, preferred_element_type=jnp.float32)
    near_sums, far = lax.optimization_barrier((near_sums, far))
    partial_sums = near_sums + jnp.einsum(
        "jkp,jpt->kt", far, far_rows, preferred_element_type=jnp.float32
    )

    filled = slot_strip >= 0
    strip_ids = jnp.maximum(slot_strip, 0)
    upper_panel = jnp.where(filled, te_panels[0][strip_ids], -1)
    lower_panel = jnp.where(filled, te_panels[1][strip_ids], -1)
    group_base = lax.axis_index("grp") * group_cols

    def select_for(side):
        first = group_base + (2 * jnp.arange(half, dtype=jnp.int32) + side) * own_cols
        panels = first[:, None] + jnp.arange(own_cols, dtype=jnp.int32)[None, :]
        upper_hits = (panels[:, :, None] == upper_panel).astype(jnp.float32)
        lower_hits = (panels[:, :, None] == lower_panel).astype(jnp.float32)
        return (upper_hits - lower_hits).astype(jnp.bfloat16)

    strength_own = jnp.einsum(
        "jkp,jps->ks", near, select_for(parity), preferred_element_type=jnp.float32
    ) + jnp.einsum("jkp,jps->ks", far, select_for(1 - parity), preferred_element_type=jnp.float32)
    strength_total = strength_own
    for shift in range(1, n_grp):
        perm = [(i, (i + shift) % n_grp) for i in range(n_grp)]
        strength_total = strength_total + lax.ppermute(strength_own, "grp", perm)
    strength = strength_total.astype(jnp.bfloat16)

    phases = phase_table(freq_index, p_size)
    eye = jnp.eye(local_slots, dtype=jnp.bfloat16)
    block_phases = (eye[:, None, :, None] * phases[None, :, None, :]).reshape(
        local_slots * 2, local_slots * p_size
    )
    wake_flat = wake_columns.reshape(local_slots * p_size, total)
    phased = jnp.dot(block_phases, wake_flat, preferred_element_type=jnp.float32)
    phased = phased.astype(jnp.bfloat16).reshape(local_slots * 2, n_dev, own_cols)
    outgoing = phased.transpose(1, 0, 2)
    arrived = lax.all_to_all(outgoing, ("row", "grp"), 0, 0, tiled=True)
    wake_right = arrived.reshape(slot_count * 2, own_cols)

    grp_index = lax.axis_index("grp")
    width = partial_sums.shape[1] // n_grp
    image_part = lax.dynamic_slice_in_dim(partial_sums, grp_index * width, width, axis=1)
    for d in range(1, n_grp):
        block = lax.dynamic_slice_in_dim(partial_sums, (grp_index ^ d) * width, width, axis=1)
        image_part = image_part + lax.ppermute(block, "grp", [(i, i ^ d) for i in range(n_grp)])

    real_part = strength[:vectors]
    imag_part = strength[vectors:]
    top = jnp.stack([real_part, -imag_part], axis=2).reshape(vectors, 2 * slot_count)
    bottom = jnp.stack([imag_part, real_part], axis=2).reshape(vectors, 2 * slot_count)
    wake_left = jnp.concatenate([top, bottom], axis=0)
    wake_part = jnp.dot(wake_left, wake_right, preferred_element_type=jnp.float32)
    image_rows = (image_part + wake_part).reshape(2, vectors, own_cols)

    local_gram = jnp.einsum("akt,alt->kl", image_rows, image_rows, precision=lax.Precision.HIGHEST)
    local_proj = jnp.einsum("akt,at->k", image_rows, residual, precision=lax.Precision.HIGHEST)
    reduced = butterfly_sum(
        butterfly_sum(jnp.concatenate([local_gram, local_proj[:, None]], axis=1), "row", n_row),
        "grp",
        n_grp,
    )
    root_count = math.sqrt(2.0 * total)
    gram_matrix = reduced[:, :vectors] / (2.0 * total)
    factor = jnp.linalg.cholesky(gram_matrix)
    q_basis = solve_rows(factor, image_rows)
    new_basis = solve_rows(factor, basis.astype(jnp.float32))
    coeffs = lax.linalg.triangular_solve(
        factor, reduced[:, vectors:], left_side=True, lower=True
    )[:, 0] / root_count
    new_residual = (
        residual
        - jnp.einsum("k,akt->at", coeffs, q_basis, precision=lax.Precision.HIGHEST) / root_count
    )
    return (q_basis, new_basis, coeffs, new_residual)


def solution(mesh):
    in_specs = (
        P(None, None, ("grp", "row")),
        P("grp", "row"),
        P(("row", "grp"), None, None),
        P(None, ("row", "grp")),
        P(),
        P(),
        P(),
    )
    out_specs = (
        P(None, None, ("row", "grp")),
        P(None, None, ("grp", "row")),
        P(),
        P(None, ("row", "grp")),
    )
    return jax.shard_map(local, mesh=mesh, in_specs=in_specs, out_specs=out_specs, check_vma=False)
```

```python
import math

import jax
import jax.numpy as jnp
from jax import lax
from jax.sharding import PartitionSpec as P


def phase_table(freq_index, panel_count):
    wavenumber = (freq_index[0].astype(jnp.float32) + 1.0) * 0.0625
    angles = (jnp.arange(panel_count, dtype=jnp.float32) + 0.5) * 0.5 * wavenumber
    return jnp.stack([jnp.cos(angles), -jnp.sin(angles)]).astype(jnp.bfloat16)


def solve_rows(factor, values):
    vectors = values.shape[1]
    width = values.shape[2]
    stacked = values.transpose(1, 0, 2).reshape(vectors, 2 * width)
    solved = lax.linalg.triangular_solve(factor, stacked, left_side=True, lower=True)
    return solved.reshape(vectors, 2, width).transpose(1, 0, 2)


def butterfly_sum(values, axis, count):
    stride = 1
    while stride < count:
        perm = [(i, i ^ stride) for i in range(count)]
        values = values + lax.ppermute(values, axis, perm)
        stride *= 2
    return values


def local(basis, body_infl, wake_columns, residual, te_panels, slot_strip, freq_index):
    n_row = lax.axis_size("row")
    n_grp = lax.axis_size("grp")
    n_dev = n_row * n_grp
    vectors = basis.shape[1]
    stacked_rows = 2 * vectors
    own_cols = basis.shape[2]
    total = own_cols * n_dev
    basis_rows = basis.reshape(stacked_rows, own_cols)
    group_cols = body_infl.shape[0]
    slot_count = slot_strip.shape[0]
    local_slots = wake_columns.shape[0]
    p_size = wake_columns.shape[1]

    row_index = lax.axis_index("row")
    half = n_row // 2
    high = row_index // 2
    parity = row_index % 2
    pieces = [basis_rows]
    for stride in range(2, n_row, 2):
        perm = [(i, i ^ stride) for i in range(n_row)]
        pieces.append(lax.ppermute(basis_rows, "row", perm))
    near = jnp.stack(pieces)[jnp.arange(half, dtype=jnp.int32) ^ high]
    far = lax.ppermute(near, "row", [(i, i ^ 1) for i in range(n_row)])
    blocks = body_infl.reshape(half, 2, own_cols, body_infl.shape[1])
    near_rows = lax.dynamic_index_in_dim(blocks, parity, 1, keepdims=False)
    far_rows = lax.dynamic_index_in_dim(blocks, 1 - parity, 1, keepdims=False)
    near_sums = jnp.einsum("jkp,jpt->kt", near, near_rows, preferred_element_type=jnp.float32)
    near_sums, far = lax.optimization_barrier((near_sums, far))
    partial_sums = near_sums + jnp.einsum(
        "jkp,jpt->kt", far, far_rows, preferred_element_type=jnp.float32
    )

    filled = slot_strip >= 0
    strip_ids = jnp.maximum(slot_strip, 0)
    upper_panel = jnp.where(filled, te_panels[0][strip_ids], -1)
    lower_panel = jnp.where(filled, te_panels[1][strip_ids], -1)
    group_base = lax.axis_index("grp") * group_cols

    def select_for(side):
        first = group_base + (2 * jnp.arange(half, dtype=jnp.int32) + side) * own_cols
        panels = first[:, None] + jnp.arange(own_cols, dtype=jnp.int32)[None, :]
        upper_hits = (panels[:, :, None] == upper_panel).astype(jnp.float32)
        lower_hits = (panels[:, :, None] == lower_panel).astype(jnp.float32)
        return (upper_hits - lower_hits).astype(jnp.bfloat16)

    strength_own = jnp.einsum(
        "jkp,jps->ks", near, select_for(parity), preferred_element_type=jnp.float32
    ) + jnp.einsum("jkp,jps->ks", far, select_for(1 - parity), preferred_element_type=jnp.float32)
    strength_total = strength_own
    for shift in range(1, n_grp):
        perm = [(i, (i + shift) % n_grp) for i in range(n_grp)]
        strength_total = strength_total + lax.ppermute(strength_own, "grp", perm)
    strength = strength_total.astype(jnp.bfloat16)

    phases = phase_table(freq_index, p_size)
    eye = jnp.eye(local_slots, dtype=jnp.bfloat16)
    block_phases = (eye[:, None, :, None] * phases[None, :, None, :]).reshape(
        local_slots * 2, local_slots * p_size
    )
    wake_flat = wake_columns.reshape(local_slots * p_size, total)
    phased = jnp.dot(block_phases, wake_flat, preferred_element_type=jnp.float32)
    phased = phased.astype(jnp.bfloat16).reshape(local_slots * 2, n_dev, own_cols)
    outgoing = phased.transpose(1, 0, 2)
    arrived = lax.all_to_all(outgoing, ("row", "grp"), 0, 0, tiled=True)
    wake_right = arrived.reshape(slot_count * 2, own_cols)

    grp_index = lax.axis_index("grp")
    width = partial_sums.shape[1] // n_grp
    image_part = lax.dynamic_slice_in_dim(partial_sums, grp_index * width, width, axis=1)
    for d in range(1, n_grp):
        block = lax.dynamic_slice_in_dim(partial_sums, (grp_index ^ d) * width, width, axis=1)
        image_part = image_part + lax.ppermute(block, "grp", [(i, i ^ d) for i in range(n_grp)])

    real_part = strength[:vectors]
    imag_part = strength[vectors:]
    top = jnp.stack([real_part, -imag_part], axis=2).reshape(vectors, 2 * slot_count)
    bottom = jnp.stack([imag_part, real_part], axis=2).reshape(vectors, 2 * slot_count)
    wake_left = jnp.concatenate([top, bottom], axis=0)
    wake_part = jnp.dot(wake_left, wake_right, preferred_element_type=jnp.float32)
    image_rows = (image_part + wake_part).reshape(2, vectors, own_cols)

    local_gram = jnp.einsum("akt,alt->kl", image_rows, image_rows, precision=lax.Precision.HIGHEST)
    local_proj = jnp.einsum("akt,at->k", image_rows, residual, precision=lax.Precision.HIGHEST)
    reduced = butterfly_sum(
        butterfly_sum(jnp.concatenate([local_gram, local_proj[:, None]], axis=1), "row", n_row),
        "grp",
        n_grp,
    )
    root_count = math.sqrt(2.0 * total)
    gram_matrix = reduced[:, :vectors] / (2.0 * total)
    factor = jnp.linalg.cholesky(gram_matrix)
    both = jnp.concatenate([image_rows, basis.astype(jnp.float32)], axis=2)
    solved = solve_rows(factor, both)
    q_basis = solved[:, :, :own_cols]
    new_basis = solved[:, :, own_cols:]
    coeffs = lax.linalg.triangular_solve(
        factor, reduced[:, vectors:], left_side=True, lower=True
    )[:, 0] / root_count
    new_residual = (
        residual
        - jnp.einsum("k,akt->at", coeffs, q_basis, precision=lax.Precision.HIGHEST) / root_count
    )
    return (q_basis, new_basis, coeffs, new_residual)


def solution(mesh):
    in_specs = (
        P(None, None, ("grp", "row")),
        P("grp", "row"),
        P(("row", "grp"), None, None),
        P(None, ("row", "grp")),
        P(),
        P(),
        P(),
    )
    out_specs = (
        P(None, None, ("row", "grp")),
        P(None, None, ("grp", "row")),
        P(),
        P(None, ("row", "grp")),
    )
    return jax.shard_map(local, mesh=mesh, in_specs=in_specs, out_specs=out_specs, check_vma=False)
```

```python
import math

import jax
import jax.numpy as jnp
from jax import lax
from jax.sharding import PartitionSpec as P


def phase_table(freq_index, panel_count):
    wavenumber = (freq_index[0].astype(jnp.float32) + 1.0) * 0.0625
    angles = (jnp.arange(panel_count, dtype=jnp.float32) + 0.5) * 0.5 * wavenumber
    return jnp.stack([jnp.cos(angles), -jnp.sin(angles)]).astype(jnp.bfloat16)


def solve_rows(factor, values):
    vectors = values.shape[1]
    width = values.shape[2]
    stacked = values.transpose(1, 0, 2).reshape(vectors, 2 * width)
    solved = lax.linalg.triangular_solve(factor, stacked, left_side=True, lower=True)
    return solved.reshape(vectors, 2, width).transpose(1, 0, 2)


def butterfly_sum(values, axis, count):
    stride = 1
    while stride < count:
        perm = [(i, i ^ stride) for i in range(count)]
        values = values + lax.ppermute(values, axis, perm)
        stride *= 2
    return values


def local(basis, body_infl, wake_columns, residual, te_panels, slot_strip, freq_index):
    n_row = lax.axis_size("row")
    n_grp = lax.axis_size("grp")
    n_dev = n_row * n_grp
    vectors = basis.shape[1]
    stacked_rows = 2 * vectors
    own_cols = basis.shape[2]
    total = own_cols * n_dev
    basis_rows = basis.reshape(stacked_rows, own_cols)
    group_cols = body_infl.shape[0]
    slot_count = slot_strip.shape[0]
    local_slots = wake_columns.shape[0]
    p_size = wake_columns.shape[1]

    row_index = lax.axis_index("row")
    half = n_row // 2
    high = row_index // 2
    parity = row_index % 2
    pieces = [basis_rows]
    for stride in range(2, n_row, 2):
        perm = [(i, i ^ stride) for i in range(n_row)]
        pieces.append(lax.ppermute(basis_rows, "row", perm))
    near = jnp.stack(pieces)[jnp.arange(half, dtype=jnp.int32) ^ high]
    far = lax.ppermute(near, "row", [(i, i ^ 1) for i in range(n_row)])
    blocks = body_infl.reshape(half, 2, own_cols, body_infl.shape[1])
    near_rows = lax.dynamic_index_in_dim(blocks, parity, 1, keepdims=False)
    far_rows = lax.dynamic_index_in_dim(blocks, 1 - parity, 1, keepdims=False)
    near_sums = jnp.einsum("jkp,jpt->kt", near, near_rows, preferred_element_type=jnp.float32)
    near_sums, far = lax.optimization_barrier((near_sums, far))
    partial_sums = near_sums + jnp.einsum(
        "jkp,jpt->kt", far, far_rows, preferred_element_type=jnp.float32
    )

    filled = slot_strip >= 0
    strip_ids = jnp.maximum(slot_strip, 0)
    upper_panel = jnp.where(filled, te_panels[0][strip_ids], -1)
    lower_panel = jnp.where(filled, te_panels[1][strip_ids], -1)
    group_base = lax.axis_index("grp") * group_cols

    def select_for(side):
        first = group_base + (2 * jnp.arange(half, dtype=jnp.int32) + side) * own_cols
        panels = first[:, None] + jnp.arange(own_cols, dtype=jnp.int32)[None, :]
        upper_hits = (panels[:, :, None] == upper_panel).astype(jnp.float32)
        lower_hits = (panels[:, :, None] == lower_panel).astype(jnp.float32)
        return (upper_hits - lower_hits).astype(jnp.bfloat16)

    strength_own = jnp.einsum(
        "jkp,jps->ks", near, select_for(parity), preferred_element_type=jnp.float32
    ) + jnp.einsum("jkp,jps->ks", far, select_for(1 - parity), preferred_element_type=jnp.float32)
    strength_total = strength_own
    for shift in range(1, n_grp):
        perm = [(i, (i + shift) % n_grp) for i in range(n_grp)]
        strength_total = strength_total + lax.ppermute(strength_own, "grp", perm)
    strength = strength_total.astype(jnp.bfloat16)

    phases = phase_table(freq_index, p_size)
    eye = jnp.eye(local_slots, dtype=jnp.bfloat16)
    block_phases = (eye[:, None, :, None] * phases[None, :, None, :]).reshape(
        local_slots * 2, local_slots * p_size
    )
    wake_flat = wake_columns.reshape(local_slots * p_size, total)
    phased = jnp.dot(block_phases, wake_flat, preferred_element_type=jnp.float32)
    phased = phased.astype(jnp.bfloat16).reshape(local_slots * 2, n_dev, own_cols)
    outgoing = phased.transpose(1, 0, 2)
    arrived = lax.all_to_all(outgoing, ("row", "grp"), 0, 0, tiled=True)
    wake_right = arrived.reshape(slot_count * 2, own_cols)

    grp_index = lax.axis_index("grp")
    width = partial_sums.shape[1] // n_grp
    image_part = lax.dynamic_slice_in_dim(partial_sums, grp_index * width, width, axis=1)
    for d in range(1, n_grp):
        block = lax.dynamic_slice_in_dim(partial_sums, (grp_index ^ d) * width, width, axis=1)
        image_part = image_part + lax.ppermute(block, "grp", [(i, i ^ d) for i in range(n_grp)])

    real_part = strength[:vectors]
    imag_part = strength[vectors:]
    top = jnp.stack([real_part, -imag_part], axis=2).reshape(vectors, 2 * slot_count)
    bottom = jnp.stack([imag_part, real_part], axis=2).reshape(vectors, 2 * slot_count)
    wake_left = jnp.concatenate([top, bottom], axis=0)
    wake_part = jnp.dot(wake_left, wake_right, preferred_element_type=jnp.float32)
    image_rows = (image_part + wake_part).reshape(2, vectors, own_cols)

    local_gram = jnp.einsum("akt,alt->kl", image_rows, image_rows, precision=lax.Precision.HIGHEST)
    local_proj = jnp.einsum("akt,at->k", image_rows, residual, precision=lax.Precision.HIGHEST)
    reduced = butterfly_sum(
        butterfly_sum(jnp.concatenate([local_gram, local_proj[:, None]], axis=1), "grp", n_grp),
        "row",
        n_row,
    )
    root_count = math.sqrt(2.0 * total)
    gram_matrix = reduced[:, :vectors] / (2.0 * total)
    factor = jnp.linalg.cholesky(gram_matrix)
    both = jnp.concatenate([image_rows, basis.astype(jnp.float32)], axis=2)
    solved = solve_rows(factor, both)
    q_basis = solved[:, :, :own_cols]
    new_basis = solved[:, :, own_cols:]
    coeffs = lax.linalg.triangular_solve(
        factor, reduced[:, vectors:], left_side=True, lower=True
    )[:, 0] / root_count
    new_residual = (
        residual
        - jnp.einsum("k,akt->at", coeffs, q_basis, precision=lax.Precision.HIGHEST) / root_count
    )
    return (q_basis, new_basis, coeffs, new_residual)


def solution(mesh):
    in_specs = (
        P(None, None, ("grp", "row")),
        P("grp", "row"),
        P(("row", "grp"), None, None),
        P(None, ("row", "grp")),
        P(),
        P(),
        P(),
    )
    out_specs = (
        P(None, None, ("row", "grp")),
        P(None, None, ("grp", "row")),
        P(),
        P(None, ("row", "grp")),
    )
    return jax.shard_map(local, mesh=mesh, in_specs=in_specs, out_specs=out_specs, check_vma=False)
```

```python
import math

import jax
import jax.numpy as jnp
from jax import lax
from jax.experimental import pallas as pl
from jax.sharding import PartitionSpec as P


def phase_table(freq_index, panel_count):
    wavenumber = (freq_index[0].astype(jnp.float32) + 1.0) * 0.0625
    angles = (jnp.arange(panel_count, dtype=jnp.float32) + 0.5) * 0.5 * wavenumber
    return jnp.stack([jnp.cos(angles), -jnp.sin(angles)]).astype(jnp.bfloat16)


def inverse_factor_kernel(gram_ref, out_ref):
    a = gram_ref[...]
    n = a.shape[0]
    rows = lax.broadcasted_iota(jnp.int32, a.shape, 0)
    cols = lax.broadcasted_iota(jnp.int32, a.shape, 1)
    factor = jnp.zeros_like(a)
    for j in range(n):
        root = jnp.sqrt(a[j:j + 1, j:j + 1])
        column = jnp.where(rows[:, :1] >= j, a[:, j:j + 1] / root, 0.0)
        row = jnp.where(cols[:1, :] >= j, a[j:j + 1, :] / root, 0.0)
        a = a - column * row
        factor = jnp.where(cols == j, column, factor)
    inverse = (rows == cols).astype(a.dtype)
    for k in range(n):
        lead = inverse[k:k + 1, :] / factor[k:k + 1, k:k + 1]
        inverse = jnp.where(rows == k, lead, inverse)
        inverse = inverse - jnp.where(rows > k, factor[:, k:k + 1], 0.0) * lead
    out_ref[...] = inverse


def inverse_factor(gram):
    return pl.pallas_call(
        inverse_factor_kernel, out_shape=jax.ShapeDtypeStruct(gram.shape, gram.dtype)
    )(gram)


def butterfly_sum(values, axis, count):
    stride = 1
    while stride < count:
        perm = [(i, i ^ stride) for i in range(count)]
        values = values + lax.ppermute(values, axis, perm)
        stride *= 2
    return values


def local(basis, body_infl, wake_columns, residual, te_panels, slot_strip, freq_index):
    n_row = lax.axis_size("row")
    n_grp = lax.axis_size("grp")
    n_dev = n_row * n_grp
    vectors = basis.shape[1]
    stacked_rows = 2 * vectors
    own_cols = basis.shape[2]
    total = own_cols * n_dev
    basis_rows = basis.reshape(stacked_rows, own_cols)
    group_cols = body_infl.shape[0]
    slot_count = slot_strip.shape[0]
    local_slots = wake_columns.shape[0]
    p_size = wake_columns.shape[1]

    row_index = lax.axis_index("row")
    half = n_row // 2
    high = row_index // 2
    parity = row_index % 2
    pieces = [basis_rows]
    for stride in range(2, n_row, 2):
        perm = [(i, i ^ stride) for i in range(n_row)]
        pieces.append(lax.ppermute(basis_rows, "row", perm))
    near = jnp.stack(pieces)[jnp.arange(half, dtype=jnp.int32) ^ high]
    far = lax.ppermute(near, "row", [(i, i ^ 1) for i in range(n_row)])
    blocks = body_infl.reshape(half, 2, own_cols, body_infl.shape[1])
    near_rows = lax.dynamic_index_in_dim(blocks, parity, 1, keepdims=False)
    far_rows = lax.dynamic_index_in_dim(blocks, 1 - parity, 1, keepdims=False)
    near_sums = jnp.einsum("jkp,jpt->kt", near, near_rows, preferred_element_type=jnp.float32)
    near_sums, far = lax.optimization_barrier((near_sums, far))
    partial_sums = near_sums + jnp.einsum(
        "jkp,jpt->kt", far, far_rows, preferred_element_type=jnp.float32
    )

    filled = slot_strip >= 0
    strip_ids = jnp.maximum(slot_strip, 0)
    upper_panel = jnp.where(filled, te_panels[0][strip_ids], -1)
    lower_panel = jnp.where(filled, te_panels[1][strip_ids], -1)
    group_base = lax.axis_index("grp") * group_cols

    def select_for(side):
        first = group_base + (2 * jnp.arange(half, dtype=jnp.int32) + side) * own_cols
        panels = first[:, None] + jnp.arange(own_cols, dtype=jnp.int32)[None, :]
        upper_hits = (panels[:, :, None] == upper_panel).astype(jnp.float32)
        lower_hits = (panels[:, :, None] == lower_panel).astype(jnp.float32)
        return (upper_hits - lower_hits).astype(jnp.bfloat16)

    strength_own = jnp.einsum(
        "jkp,jps->ks", near, select_for(parity), preferred_element_type=jnp.float32
    ) + jnp.einsum("jkp,jps->ks", far, select_for(1 - parity), preferred_element_type=jnp.float32)
    strength_total = strength_own
    for shift in range(1, n_grp):
        perm = [(i, (i + shift) % n_grp) for i in range(n_grp)]
        strength_total = strength_total + lax.ppermute(strength_own, "grp", perm)
    strength = strength_total.astype(jnp.bfloat16)

    phases = phase_table(freq_index, p_size)
    eye = jnp.eye(local_slots, dtype=jnp.bfloat16)
    block_phases = (eye[:, None, :, None] * phases[None, :, None, :]).reshape(
        local_slots * 2, local_slots * p_size
    )
    wake_flat = wake_columns.reshape(local_slots * p_size, total)
    phased = jnp.dot(block_phases, wake_flat, preferred_element_type=jnp.float32)
    phased = phased.astype(jnp.bfloat16).reshape(local_slots * 2, n_dev, own_cols)
    outgoing = phased.transpose(1, 0, 2)
    arrived = lax.all_to_all(outgoing, ("row", "grp"), 0, 0, tiled=True)
    wake_right = arrived.reshape(slot_count * 2, own_cols)

    grp_index = lax.axis_index("grp")
    width = partial_sums.shape[1] // n_grp
    image_part = lax.dynamic_slice_in_dim(partial_sums, grp_index * width, width, axis=1)
    for d in range(1, n_grp):
        block = lax.dynamic_slice_in_dim(partial_sums, (grp_index ^ d) * width, width, axis=1)
        image_part = image_part + lax.ppermute(block, "grp", [(i, i ^ d) for i in range(n_grp)])

    real_part = strength[:vectors]
    imag_part = strength[vectors:]
    top = jnp.stack([real_part, -imag_part], axis=2).reshape(vectors, 2 * slot_count)
    bottom = jnp.stack([imag_part, real_part], axis=2).reshape(vectors, 2 * slot_count)
    wake_left = jnp.concatenate([top, bottom], axis=0)
    wake_part = jnp.dot(wake_left, wake_right, preferred_element_type=jnp.float32)
    image_rows = (image_part + wake_part).reshape(2, vectors, own_cols)

    local_gram = jnp.einsum("akt,alt->kl", image_rows, image_rows, precision=lax.Precision.HIGHEST)
    local_proj = jnp.einsum("akt,at->k", image_rows, residual, precision=lax.Precision.HIGHEST)
    reduced = butterfly_sum(
        butterfly_sum(jnp.concatenate([local_gram, local_proj[:, None]], axis=1), "row", n_row),
        "grp",
        n_grp,
    )
    root_count = math.sqrt(2.0 * total)
    gram_matrix = reduced[:, :vectors] / (2.0 * total)
    symmetric = (gram_matrix + gram_matrix.T) / 2.0
    inverse = inverse_factor(symmetric)
    both = jnp.concatenate([image_rows, basis.astype(jnp.float32)], axis=2)
    solved = jnp.einsum("kl,alt->akt", inverse, both, precision=lax.Precision.HIGHEST)
    q_basis = solved[:, :, :own_cols]
    new_basis = solved[:, :, own_cols:]
    coeffs = jnp.dot(inverse, reduced[:, vectors], precision=lax.Precision.HIGHEST) / root_count
    new_residual = (
        residual
        - jnp.einsum("k,akt->at", coeffs, q_basis, precision=lax.Precision.HIGHEST) / root_count
    )
    return (q_basis, new_basis, coeffs, new_residual)


def solution(mesh):
    in_specs = (
        P(None, None, ("grp", "row")),
        P("grp", "row"),
        P(("row", "grp"), None, None),
        P(None, ("row", "grp")),
        P(),
        P(),
        P(),
    )
    out_specs = (
        P(None, None, ("row", "grp")),
        P(None, None, ("grp", "row")),
        P(),
        P(None, ("row", "grp")),
    )
    return jax.shard_map(local, mesh=mesh, in_specs=in_specs, out_specs=out_specs, check_vma=False)
```

```python
import math

import jax
import jax.numpy as jnp
from jax import lax
from jax.experimental import pallas as pl
from jax.experimental.pallas import tpu as pltpu
from jax.sharding import PartitionSpec as P


def phase_table(freq_index, panel_count):
    wavenumber = (freq_index[0].astype(jnp.float32) + 1.0) * 0.0625
    angles = (jnp.arange(panel_count, dtype=jnp.float32) + 0.5) * 0.5 * wavenumber
    return jnp.stack([jnp.cos(angles), -jnp.sin(angles)]).astype(jnp.bfloat16)


def inverse_factor_kernel(gram_ref, out_ref, work_ref):
    n = gram_ref.shape[0]
    work_ref[...] = gram_ref[...]
    rows = lax.broadcasted_iota(jnp.int32, (n, n), 0)
    cols = lax.broadcasted_iota(jnp.int32, (n, n), 1)
    out_ref[...] = (rows == cols).astype(out_ref.dtype)
    lane = lax.broadcasted_iota(jnp.int32, (1, n), 1)
    for j in range(n):
        top = (j // 8) * 8
        below = lax.broadcasted_iota(jnp.int32, (n - top, 1), 0) + top
        scale = 1.0 / jnp.sqrt(work_ref[j:j + 1, j:j + 1])
        column = jnp.where(below >= j, work_ref[top:, j:j + 1] * scale, 0.0)
        row = jnp.where(lane >= j, work_ref[j:j + 1, :] * scale, 0.0)
        work_ref[top:, :] = work_ref[top:, :] - column * row
        lead = out_ref[j:j + 1, :] * scale
        out_ref[top:, :] = jnp.where(below == j, lead, out_ref[top:, :] - column * lead)


def inverse_factor(gram):
    return pl.pallas_call(
        inverse_factor_kernel,
        out_shape=jax.ShapeDtypeStruct(gram.shape, gram.dtype),
        scratch_shapes=[pltpu.VMEM(gram.shape, gram.dtype)],
    )(gram)


def butterfly_sum(values, axis, count):
    stride = 1
    while stride < count:
        perm = [(i, i ^ stride) for i in range(count)]
        values = values + lax.ppermute(values, axis, perm)
        stride *= 2
    return values


def local(basis, body_infl, wake_columns, residual, te_panels, slot_strip, freq_index):
    n_row = lax.axis_size("row")
    n_grp = lax.axis_size("grp")
    n_dev = n_row * n_grp
    vectors = basis.shape[1]
    stacked_rows = 2 * vectors
    own_cols = basis.shape[2]
    total = own_cols * n_dev
    basis_rows = basis.reshape(stacked_rows, own_cols)
    group_cols = body_infl.shape[0]
    slot_count = slot_strip.shape[0]
    local_slots = wake_columns.shape[0]
    p_size = wake_columns.shape[1]

    row_index = lax.axis_index("row")
    half = n_row // 2
    high = row_index // 2
    parity = row_index % 2
    pieces = [basis_rows]
    for stride in range(2, n_row, 2):
        perm = [(i, i ^ stride) for i in range(n_row)]
        pieces.append(lax.ppermute(basis_rows, "row", perm))
    near = jnp.stack(pieces)[jnp.arange(half, dtype=jnp.int32) ^ high]
    far = lax.ppermute(near, "row", [(i, i ^ 1) for i in range(n_row)])
    blocks = body_infl.reshape(half, 2, own_cols, body_infl.shape[1])
    near_rows = lax.dynamic_index_in_dim(blocks, parity, 1, keepdims=False)
    far_rows = lax.dynamic_index_in_dim(blocks, 1 - parity, 1, keepdims=False)
    near_sums = jnp.einsum("jkp,jpt->kt", near, near_rows, preferred_element_type=jnp.float32)
    near_sums, far = lax.optimization_barrier((near_sums, far))
    partial_sums = near_sums + jnp.einsum(
        "jkp,jpt->kt", far, far_rows, preferred_element_type=jnp.float32
    )

    filled = slot_strip >= 0
    strip_ids = jnp.maximum(slot_strip, 0)
    upper_panel = jnp.where(filled, te_panels[0][strip_ids], -1)
    lower_panel = jnp.where(filled, te_panels[1][strip_ids], -1)
    group_base = lax.axis_index("grp") * group_cols

    def select_for(side):
        first = group_base + (2 * jnp.arange(half, dtype=jnp.int32) + side) * own_cols
        panels = first[:, None] + jnp.arange(own_cols, dtype=jnp.int32)[None, :]
        upper_hits = (panels[:, :, None] == upper_panel).astype(jnp.float32)
        lower_hits = (panels[:, :, None] == lower_panel).astype(jnp.float32)
        return (upper_hits - lower_hits).astype(jnp.bfloat16)

    strength_own = jnp.einsum(
        "jkp,jps->ks", near, select_for(parity), preferred_element_type=jnp.float32
    ) + jnp.einsum("jkp,jps->ks", far, select_for(1 - parity), preferred_element_type=jnp.float32)
    strength_total = strength_own
    for shift in range(1, n_grp):
        perm = [(i, (i + shift) % n_grp) for i in range(n_grp)]
        strength_total = strength_total + lax.ppermute(strength_own, "grp", perm)
    strength = strength_total.astype(jnp.bfloat16)

    phases = phase_table(freq_index, p_size)
    eye = jnp.eye(local_slots, dtype=jnp.bfloat16)
    block_phases = (eye[:, None, :, None] * phases[None, :, None, :]).reshape(
        local_slots * 2, local_slots * p_size
    )
    wake_flat = wake_columns.reshape(local_slots * p_size, total)
    phased = jnp.dot(block_phases, wake_flat, preferred_element_type=jnp.float32)
    phased = phased.astype(jnp.bfloat16).reshape(local_slots * 2, n_dev, own_cols)
    outgoing = phased.transpose(1, 0, 2)
    arrived = lax.all_to_all(outgoing, ("row", "grp"), 0, 0, tiled=True)
    wake_right = arrived.reshape(slot_count * 2, own_cols)

    grp_index = lax.axis_index("grp")
    width = partial_sums.shape[1] // n_grp
    image_part = lax.dynamic_slice_in_dim(partial_sums, grp_index * width, width, axis=1)
    for d in range(1, n_grp):
        block = lax.dynamic_slice_in_dim(partial_sums, (grp_index ^ d) * width, width, axis=1)
        image_part = image_part + lax.ppermute(block, "grp", [(i, i ^ d) for i in range(n_grp)])

    real_part = strength[:vectors]
    imag_part = strength[vectors:]
    top = jnp.stack([real_part, -imag_part], axis=2).reshape(vectors, 2 * slot_count)
    bottom = jnp.stack([imag_part, real_part], axis=2).reshape(vectors, 2 * slot_count)
    wake_left = jnp.concatenate([top, bottom], axis=0)
    wake_part = jnp.dot(wake_left, wake_right, preferred_element_type=jnp.float32)
    image_rows = (image_part + wake_part).reshape(2, vectors, own_cols)

    local_gram = jnp.einsum("akt,alt->kl", image_rows, image_rows, precision=lax.Precision.HIGHEST)
    local_proj = jnp.einsum("akt,at->k", image_rows, residual, precision=lax.Precision.HIGHEST)
    reduced = butterfly_sum(
        butterfly_sum(jnp.concatenate([local_gram, local_proj[:, None]], axis=1), "row", n_row),
        "grp",
        n_grp,
    )
    root_count = math.sqrt(2.0 * total)
    gram_matrix = reduced[:, :vectors] / (2.0 * total)
    symmetric = (gram_matrix + gram_matrix.T) / 2.0
    inverse = inverse_factor(symmetric)
    both = jnp.concatenate([image_rows, basis.astype(jnp.float32)], axis=2)
    solved = jnp.einsum("kl,alt->akt", inverse, both, precision=lax.Precision.HIGHEST)
    q_basis = solved[:, :, :own_cols]
    new_basis = solved[:, :, own_cols:]
    coeffs = jnp.dot(inverse, reduced[:, vectors], precision=lax.Precision.HIGHEST) / root_count
    new_residual = (
        residual
        - jnp.einsum("k,akt->at", coeffs, q_basis, precision=lax.Precision.HIGHEST) / root_count
    )
    return (q_basis, new_basis, coeffs, new_residual)


def solution(mesh):
    in_specs = (
        P(None, None, ("grp", "row")),
        P("grp", "row"),
        P(("row", "grp"), None, None),
        P(None, ("row", "grp")),
        P(),
        P(),
        P(),
    )
    out_specs = (
        P(None, None, ("row", "grp")),
        P(None, None, ("grp", "row")),
        P(),
        P(None, ("row", "grp")),
    )
    return jax.shard_map(local, mesh=mesh, in_specs=in_specs, out_specs=out_specs, check_vma=False)
```

```python
import math

import jax
import jax.numpy as jnp
from jax import lax
from jax.experimental import pallas as pl
from jax.sharding import PartitionSpec as P


def phase_table(freq_index, panel_count):
    wavenumber = (freq_index[0].astype(jnp.float32) + 1.0) * 0.0625
    angles = (jnp.arange(panel_count, dtype=jnp.float32) + 0.5) * 0.5 * wavenumber
    return jnp.stack([jnp.cos(angles), -jnp.sin(angles)]).astype(jnp.bfloat16)


def inverse_factor_kernel(gram_ref, out_ref):
    work = gram_ref[...]
    n = work.shape[0]
    rows = lax.broadcasted_iota(jnp.int32, work.shape, 0)
    cols = lax.broadcasted_iota(jnp.int32, work.shape, 1)
    inverse = (rows == cols).astype(work.dtype)
    for j in range(n):
        scale = 1.0 / jnp.sqrt(work[j:j + 1, j:j + 1])
        column = jnp.where(rows[:, :1] >= j, work[:, j:j + 1] * scale, 0.0)
        row = jnp.where(cols[:1, :] >= j, work[j:j + 1, :] * scale, 0.0)
        work = work - column * row
        lead = inverse[j:j + 1, :] * scale
        inverse = jnp.where(rows == j, lead, inverse - column * lead)
    out_ref[...] = inverse


def inverse_factor(gram):
    return pl.pallas_call(
        inverse_factor_kernel, out_shape=jax.ShapeDtypeStruct(gram.shape, gram.dtype)
    )(gram)


def butterfly_sum(values, axis, count):
    stride = 1
    while stride < count:
        perm = [(i, i ^ stride) for i in range(count)]
        values = values + lax.ppermute(values, axis, perm)
        stride *= 2
    return values


def local(basis, body_infl, wake_columns, residual, te_panels, slot_strip, freq_index):
    n_row = lax.axis_size("row")
    n_grp = lax.axis_size("grp")
    n_dev = n_row * n_grp
    vectors = basis.shape[1]
    stacked_rows = 2 * vectors
    own_cols = basis.shape[2]
    total = own_cols * n_dev
    basis_rows = basis.reshape(stacked_rows, own_cols)
    group_cols = body_infl.shape[0]
    slot_count = slot_strip.shape[0]
    local_slots = wake_columns.shape[0]
    p_size = wake_columns.shape[1]

    row_index = lax.axis_index("row")
    half = n_row // 2
    high = row_index // 2
    parity = row_index % 2
    pieces = [basis_rows]
    for stride in range(2, n_row, 2):
        perm = [(i, i ^ stride) for i in range(n_row)]
        pieces.append(lax.ppermute(basis_rows, "row", perm))
    near = jnp.stack(pieces)[jnp.arange(half, dtype=jnp.int32) ^ high]
    far = lax.ppermute(near, "row", [(i, i ^ 1) for i in range(n_row)])
    blocks = body_infl.reshape(half, 2, own_cols, body_infl.shape[1])
    near_rows = lax.dynamic_index_in_dim(blocks, parity, 1, keepdims=False)
    far_rows = lax.dynamic_index_in_dim(blocks, 1 - parity, 1, keepdims=False)
    near_sums = jnp.einsum("jkp,jpt->kt", near, near_rows, preferred_element_type=jnp.float32)
    near_sums, far = lax.optimization_barrier((near_sums, far))
    partial_sums = near_sums + jnp.einsum(
        "jkp,jpt->kt", far, far_rows, preferred_element_type=jnp.float32
    )

    filled = slot_strip >= 0
    strip_ids = jnp.maximum(slot_strip, 0)
    upper_panel = jnp.where(filled, te_panels[0][strip_ids], -1)
    lower_panel = jnp.where(filled, te_panels[1][strip_ids], -1)
    group_base = lax.axis_index("grp") * group_cols

    def select_for(side):
        first = group_base + (2 * jnp.arange(half, dtype=jnp.int32) + side) * own_cols
        panels = first[:, None] + jnp.arange(own_cols, dtype=jnp.int32)[None, :]
        upper_hits = (panels[:, :, None] == upper_panel).astype(jnp.float32)
        lower_hits = (panels[:, :, None] == lower_panel).astype(jnp.float32)
        return (upper_hits - lower_hits).astype(jnp.bfloat16)

    strength_own = jnp.einsum(
        "jkp,jps->ks", near, select_for(parity), preferred_element_type=jnp.float32
    ) + jnp.einsum("jkp,jps->ks", far, select_for(1 - parity), preferred_element_type=jnp.float32)
    strength_total = strength_own
    for shift in range(1, n_grp):
        perm = [(i, (i + shift) % n_grp) for i in range(n_grp)]
        strength_total = strength_total + lax.ppermute(strength_own, "grp", perm)
    strength = strength_total.astype(jnp.bfloat16)

    phases = phase_table(freq_index, p_size)
    eye = jnp.eye(local_slots, dtype=jnp.bfloat16)
    block_phases = (eye[:, None, :, None] * phases[None, :, None, :]).reshape(
        local_slots * 2, local_slots * p_size
    )
    wake_flat = wake_columns.reshape(local_slots * p_size, total)
    phased = jnp.dot(block_phases, wake_flat, preferred_element_type=jnp.float32)
    phased = phased.astype(jnp.bfloat16).reshape(local_slots * 2, n_dev, own_cols)
    outgoing = phased.transpose(1, 0, 2)
    arrived = lax.all_to_all(outgoing, ("row", "grp"), 0, 0, tiled=True)
    wake_right = arrived.reshape(slot_count * 2, own_cols)

    grp_index = lax.axis_index("grp")
    width = partial_sums.shape[1] // n_grp
    image_part = lax.dynamic_slice_in_dim(partial_sums, grp_index * width, width, axis=1)
    for d in range(1, n_grp):
        block = lax.dynamic_slice_in_dim(partial_sums, (grp_index ^ d) * width, width, axis=1)
        image_part = image_part + lax.ppermute(block, "grp", [(i, i ^ d) for i in range(n_grp)])

    real_part = strength[:vectors]
    imag_part = strength[vectors:]
    top = jnp.stack([real_part, -imag_part], axis=2).reshape(vectors, 2 * slot_count)
    bottom = jnp.stack([imag_part, real_part], axis=2).reshape(vectors, 2 * slot_count)
    wake_left = jnp.concatenate([top, bottom], axis=0)
    wake_part = jnp.dot(wake_left, wake_right, preferred_element_type=jnp.float32)
    image_rows = (image_part + wake_part).reshape(2, vectors, own_cols)

    local_gram = jnp.einsum("akt,alt->kl", image_rows, image_rows, precision=lax.Precision.HIGHEST)
    local_proj = jnp.einsum("akt,at->k", image_rows, residual, precision=lax.Precision.HIGHEST)
    reduced = butterfly_sum(
        butterfly_sum(jnp.concatenate([local_gram, local_proj[:, None]], axis=1), "row", n_row),
        "grp",
        n_grp,
    )
    root_count = math.sqrt(2.0 * total)
    gram_matrix = reduced[:, :vectors] / (2.0 * total)
    symmetric = (gram_matrix + gram_matrix.T) / 2.0
    inverse = inverse_factor(symmetric)
    both = jnp.concatenate([image_rows, basis.astype(jnp.float32)], axis=2)
    solved = jnp.einsum("kl,alt->akt", inverse, both, precision=lax.Precision.HIGHEST)
    q_basis = solved[:, :, :own_cols]
    new_basis = solved[:, :, own_cols:]
    coeffs = jnp.dot(inverse, reduced[:, vectors], precision=lax.Precision.HIGHEST) / root_count
    new_residual = (
        residual
        - jnp.einsum("k,akt->at", coeffs, q_basis, precision=lax.Precision.HIGHEST) / root_count
    )
    return (q_basis, new_basis, coeffs, new_residual)


def solution(mesh):
    in_specs = (
        P(None, None, ("grp", "row")),
        P("grp", "row"),
        P(("row", "grp"), None, None),
        P(None, ("row", "grp")),
        P(),
        P(),
        P(),
    )
    out_specs = (
        P(None, None, ("row", "grp")),
        P(None, None, ("grp", "row")),
        P(),
        P(None, ("row", "grp")),
    )
    return jax.shard_map(local, mesh=mesh, in_specs=in_specs, out_specs=out_specs, check_vma=False)
```

```python
import math

import jax
import jax.numpy as jnp
from jax import lax
from jax.experimental import pallas as pl
from jax.sharding import PartitionSpec as P


def phase_table(freq_index, panel_count):
    wavenumber = (freq_index[0].astype(jnp.float32) + 1.0) * 0.0625
    angles = (jnp.arange(panel_count, dtype=jnp.float32) + 0.5) * 0.5 * wavenumber
    return jnp.stack([jnp.cos(angles), -jnp.sin(angles)]).astype(jnp.bfloat16)


def inverse_factor_kernel(gram_ref, out_ref):
    work = gram_ref[...]
    n = work.shape[0]
    rows = lax.broadcasted_iota(jnp.int32, work.shape, 0)
    cols = lax.broadcasted_iota(jnp.int32, work.shape, 1)
    inverse = (rows == cols).astype(work.dtype)
    j = 0
    while j < n:
        scale = 1.0 / jnp.sqrt(work[j:j + 1, j:j + 1])
        column = jnp.where(rows[:, :1] >= j, work[:, j:j + 1] * scale, 0.0)
        row = jnp.where(cols[:1, :] >= j, work[j:j + 1, :] * scale, 0.0)
        lead = inverse[j:j + 1, :] * scale
        if j + 1 < n:
            cross = work[j + 1:j + 2, j:j + 1] * scale
            scale2 = 1.0 / jnp.sqrt(work[j + 1:j + 2, j + 1:j + 2] - cross * cross)
            column2 = jnp.where(
                rows[:, :1] >= j + 1, (work[:, j + 1:j + 2] - column * cross) * scale2, 0.0
            )
            row2 = jnp.where(cols[:1, :] >= j + 1, (work[j + 1:j + 2, :] - row * cross) * scale2, 0.0)
            lead2 = (inverse[j + 1:j + 2, :] - cross * lead) * scale2
            work = work - column * row - column2 * row2
            rest = inverse - column * lead - column2 * lead2
            inverse = jnp.where(rows == j, lead, jnp.where(rows == j + 1, lead2, rest))
            j += 2
        else:
            work = work - column * row
            inverse = jnp.where(rows == j, lead, inverse - column * lead)
            j += 1
    out_ref[...] = inverse


def inverse_factor(gram):
    return pl.pallas_call(
        inverse_factor_kernel, out_shape=jax.ShapeDtypeStruct(gram.shape, gram.dtype)
    )(gram)


def butterfly_sum(values, axis, count):
    stride = 1
    while stride < count:
        perm = [(i, i ^ stride) for i in range(count)]
        values = values + lax.ppermute(values, axis, perm)
        stride *= 2
    return values


def local(basis, body_infl, wake_columns, residual, te_panels, slot_strip, freq_index):
    n_row = lax.axis_size("row")
    n_grp = lax.axis_size("grp")
    n_dev = n_row * n_grp
    vectors = basis.shape[1]
    stacked_rows = 2 * vectors
    own_cols = basis.shape[2]
    total = own_cols * n_dev
    basis_rows = basis.reshape(stacked_rows, own_cols)
    group_cols = body_infl.shape[0]
    slot_count = slot_strip.shape[0]
    local_slots = wake_columns.shape[0]
    p_size = wake_columns.shape[1]

    row_index = lax.axis_index("row")
    half = n_row // 2
    high = row_index // 2
    parity = row_index % 2
    pieces = [basis_rows]
    for stride in range(2, n_row, 2):
        perm = [(i, i ^ stride) for i in range(n_row)]
        pieces.append(lax.ppermute(basis_rows, "row", perm))
    near = jnp.stack(pieces)[jnp.arange(half, dtype=jnp.int32) ^ high]
    far = lax.ppermute(near, "row", [(i, i ^ 1) for i in range(n_row)])
    blocks = body_infl.reshape(half, 2, own_cols, body_infl.shape[1])
    near_rows = lax.dynamic_index_in_dim(blocks, parity, 1, keepdims=False)
    far_rows = lax.dynamic_index_in_dim(blocks, 1 - parity, 1, keepdims=False)
    near_sums = jnp.einsum("jkp,jpt->kt", near, near_rows, preferred_element_type=jnp.float32)
    near_sums, far = lax.optimization_barrier((near_sums, far))
    partial_sums = near_sums + jnp.einsum(
        "jkp,jpt->kt", far, far_rows, preferred_element_type=jnp.float32
    )

    filled = slot_strip >= 0
    strip_ids = jnp.maximum(slot_strip, 0)
    upper_panel = jnp.where(filled, te_panels[0][strip_ids], -1)
    lower_panel = jnp.where(filled, te_panels[1][strip_ids], -1)
    group_base = lax.axis_index("grp") * group_cols

    def select_for(side):
        first = group_base + (2 * jnp.arange(half, dtype=jnp.int32) + side) * own_cols
        panels = first[:, None] + jnp.arange(own_cols, dtype=jnp.int32)[None, :]
        upper_hits = (panels[:, :, None] == upper_panel).astype(jnp.float32)
        lower_hits = (panels[:, :, None] == lower_panel).astype(jnp.float32)
        return (upper_hits - lower_hits).astype(jnp.bfloat16)

    strength_own = jnp.einsum(
        "jkp,jps->ks", near, select_for(parity), preferred_element_type=jnp.float32
    ) + jnp.einsum("jkp,jps->ks", far, select_for(1 - parity), preferred_element_type=jnp.float32)
    strength_total = strength_own
    for shift in range(1, n_grp):
        perm = [(i, (i + shift) % n_grp) for i in range(n_grp)]
        strength_total = strength_total + lax.ppermute(strength_own, "grp", perm)
    strength = strength_total.astype(jnp.bfloat16)

    phases = phase_table(freq_index, p_size)
    eye = jnp.eye(local_slots, dtype=jnp.bfloat16)
    block_phases = (eye[:, None, :, None] * phases[None, :, None, :]).reshape(
        local_slots * 2, local_slots * p_size
    )
    wake_flat = wake_columns.reshape(local_slots * p_size, total)
    phased = jnp.dot(block_phases, wake_flat, preferred_element_type=jnp.float32)
    phased = phased.astype(jnp.bfloat16).reshape(local_slots * 2, n_dev, own_cols)
    outgoing = phased.transpose(1, 0, 2)
    arrived = lax.all_to_all(outgoing, ("row", "grp"), 0, 0, tiled=True)
    wake_right = arrived.reshape(slot_count * 2, own_cols)

    grp_index = lax.axis_index("grp")
    width = partial_sums.shape[1] // n_grp
    image_part = lax.dynamic_slice_in_dim(partial_sums, grp_index * width, width, axis=1)
    for d in range(1, n_grp):
        block = lax.dynamic_slice_in_dim(partial_sums, (grp_index ^ d) * width, width, axis=1)
        image_part = image_part + lax.ppermute(block, "grp", [(i, i ^ d) for i in range(n_grp)])

    real_part = strength[:vectors]
    imag_part = strength[vectors:]
    top = jnp.stack([real_part, -imag_part], axis=2).reshape(vectors, 2 * slot_count)
    bottom = jnp.stack([imag_part, real_part], axis=2).reshape(vectors, 2 * slot_count)
    wake_left = jnp.concatenate([top, bottom], axis=0)
    wake_part = jnp.dot(wake_left, wake_right, preferred_element_type=jnp.float32)
    image_rows = (image_part + wake_part).reshape(2, vectors, own_cols)

    local_gram = jnp.einsum("akt,alt->kl", image_rows, image_rows, precision=lax.Precision.HIGHEST)
    local_proj = jnp.einsum("akt,at->k", image_rows, residual, precision=lax.Precision.HIGHEST)
    reduced = butterfly_sum(
        butterfly_sum(jnp.concatenate([local_gram, local_proj[:, None]], axis=1), "row", n_row),
        "grp",
        n_grp,
    )
    root_count = math.sqrt(2.0 * total)
    gram_matrix = reduced[:, :vectors] / (2.0 * total)
    symmetric = (gram_matrix + gram_matrix.T) / 2.0
    inverse = inverse_factor(symmetric)
    both = jnp.concatenate([image_rows, basis.astype(jnp.float32)], axis=2)
    solved = jnp.einsum("kl,alt->akt", inverse, both, precision=lax.Precision.HIGHEST)
    q_basis = solved[:, :, :own_cols]
    new_basis = solved[:, :, own_cols:]
    coeffs = jnp.dot(inverse, reduced[:, vectors], precision=lax.Precision.HIGHEST) / root_count
    new_residual = (
        residual
        - jnp.einsum("k,akt->at", coeffs, q_basis, precision=lax.Precision.HIGHEST) / root_count
    )
    return (q_basis, new_basis, coeffs, new_residual)


def solution(mesh):
    in_specs = (
        P(None, None, ("grp", "row")),
        P("grp", "row"),
        P(("row", "grp"), None, None),
        P(None, ("row", "grp")),
        P(),
        P(),
        P(),
    )
    out_specs = (
        P(None, None, ("row", "grp")),
        P(None, None, ("grp", "row")),
        P(),
        P(None, ("row", "grp")),
    )
    return jax.shard_map(local, mesh=mesh, in_specs=in_specs, out_specs=out_specs, check_vma=False)
```

```python
import math

import jax
import jax.numpy as jnp
from jax import lax
from jax.experimental import pallas as pl
from jax.sharding import PartitionSpec as P


def phase_table(freq_index, panel_count):
    wavenumber = (freq_index[0].astype(jnp.float32) + 1.0) * 0.0625
    angles = (jnp.arange(panel_count, dtype=jnp.float32) + 0.5) * 0.5 * wavenumber
    return jnp.stack([jnp.cos(angles), -jnp.sin(angles)]).astype(jnp.bfloat16)


def inverse_factor_kernel(gram_ref, out_ref):
    work = gram_ref[...]
    n = work.shape[0]
    rows = lax.broadcasted_iota(jnp.int32, work.shape, 0)
    cols = lax.broadcasted_iota(jnp.int32, work.shape, 1)
    inverse = (rows == cols).astype(work.dtype)
    for j in range(n):
        scale = 1.0 / jnp.sqrt(work[j:j + 1, j:j + 1])
        column = jnp.where(rows[:, :1] >= j, work[:, j:j + 1] * scale, 0.0)
        row = jnp.where(cols[:1, :] >= j, work[j:j + 1, :] * scale, 0.0)
        work = work - column * row
        lead = inverse[j:j + 1, :] * scale
        inverse = jnp.where(rows == j, lead, inverse - column * lead)
    out_ref[...] = inverse


def inverse_factor(gram):
    return pl.pallas_call(
        inverse_factor_kernel, out_shape=jax.ShapeDtypeStruct(gram.shape, gram.dtype)
    )(gram)


def butterfly_sum(values, axis, count):
    stride = 1
    while stride < count:
        perm = [(i, i ^ stride) for i in range(count)]
        values = values + lax.ppermute(values, axis, perm)
        stride *= 2
    return values


def local(basis, body_infl, wake_columns, residual, te_panels, slot_strip, freq_index):
    n_row = lax.axis_size("row")
    n_grp = lax.axis_size("grp")
    n_dev = n_row * n_grp
    vectors = basis.shape[1]
    stacked_rows = 2 * vectors
    own_cols = basis.shape[2]
    total = own_cols * n_dev
    basis_rows = basis.reshape(stacked_rows, own_cols)
    group_cols = body_infl.shape[0]
    slot_count = slot_strip.shape[0]
    local_slots = wake_columns.shape[0]
    p_size = wake_columns.shape[1]

    row_index = lax.axis_index("row")
    half = n_row // 2
    high = row_index // 2
    parity = row_index % 2
    pieces = [basis_rows]
    for stride in range(2, n_row, 2):
        perm = [(i, i ^ stride) for i in range(n_row)]
        pieces.append(lax.ppermute(basis_rows, "row", perm))
    near = jnp.stack(pieces)[jnp.arange(half, dtype=jnp.int32) ^ high]
    far = lax.ppermute(near, "row", [(i, i ^ 1) for i in range(n_row)])
    blocks = body_infl.reshape(half, 2, own_cols, body_infl.shape[1])
    near_rows = lax.dynamic_index_in_dim(blocks, parity, 1, keepdims=False)
    far_rows = lax.dynamic_index_in_dim(blocks, 1 - parity, 1, keepdims=False)
    near_sums = jnp.einsum("jkp,jpt->kt", near, near_rows, preferred_element_type=jnp.float32)
    near_sums, far = lax.optimization_barrier((near_sums, far))
    partial_sums = near_sums + jnp.einsum(
        "jkp,jpt->kt", far, far_rows, preferred_element_type=jnp.float32
    )

    filled = slot_strip >= 0
    strip_ids = jnp.maximum(slot_strip, 0)
    upper_panel = jnp.where(filled, te_panels[0][strip_ids], -1)
    lower_panel = jnp.where(filled, te_panels[1][strip_ids], -1)
    group_base = lax.axis_index("grp") * group_cols

    def select_for(side):
        first = group_base + (2 * jnp.arange(half, dtype=jnp.int32) + side) * own_cols
        panels = first[:, None] + jnp.arange(own_cols, dtype=jnp.int32)[None, :]
        upper_hits = (panels[:, :, None] == upper_panel).astype(jnp.float32)
        lower_hits = (panels[:, :, None] == lower_panel).astype(jnp.float32)
        return (upper_hits - lower_hits).astype(jnp.bfloat16)

    strength_own = jnp.einsum(
        "jkp,jps->ks", near, select_for(parity), preferred_element_type=jnp.float32
    ) + jnp.einsum("jkp,jps->ks", far, select_for(1 - parity), preferred_element_type=jnp.float32)
    strength_total = strength_own
    for shift in range(1, n_grp):
        perm = [(i, (i + shift) % n_grp) for i in range(n_grp)]
        strength_total = strength_total + lax.ppermute(strength_own, "grp", perm)
    strength = strength_total.astype(jnp.bfloat16)

    phases = phase_table(freq_index, p_size)
    eye = jnp.eye(local_slots, dtype=jnp.bfloat16)
    block_phases = (eye[:, None, :, None] * phases[None, :, None, :]).reshape(
        local_slots * 2, local_slots * p_size
    )
    wake_flat = wake_columns.reshape(local_slots * p_size, total)
    phased = jnp.dot(block_phases, wake_flat, preferred_element_type=jnp.float32)
    phased = phased.astype(jnp.bfloat16).reshape(local_slots * 2, n_dev, own_cols)
    outgoing = phased.transpose(1, 0, 2)
    arrived = lax.all_to_all(outgoing, ("row", "grp"), 0, 0, tiled=True)
    wake_right = arrived.reshape(slot_count * 2, own_cols)

    grp_index = lax.axis_index("grp")
    width = partial_sums.shape[1] // n_grp
    image_part = lax.dynamic_slice_in_dim(partial_sums, grp_index * width, width, axis=1)
    for d in range(1, n_grp):
        block = lax.dynamic_slice_in_dim(partial_sums, (grp_index ^ d) * width, width, axis=1)
        image_part = image_part + lax.ppermute(block, "grp", [(i, i ^ d) for i in range(n_grp)])

    real_part = strength[:vectors]
    imag_part = strength[vectors:]
    top = jnp.stack([real_part, -imag_part], axis=2).reshape(vectors, 2 * slot_count)
    bottom = jnp.stack([imag_part, real_part], axis=2).reshape(vectors, 2 * slot_count)
    wake_left = jnp.concatenate([top, bottom], axis=0)
    wake_part = jnp.dot(wake_left, wake_right, preferred_element_type=jnp.float32)
    image_rows = (image_part + wake_part).reshape(2, vectors, own_cols)

    local_gram = jnp.einsum("akt,alt->kl", image_rows, image_rows, precision=lax.Precision.HIGHEST)
    local_proj = jnp.einsum("akt,at->k", image_rows, residual, precision=lax.Precision.HIGHEST)
    reduced = butterfly_sum(
        butterfly_sum(jnp.concatenate([local_gram, local_proj[:, None]], axis=1), "row", n_row),
        "grp",
        n_grp,
    )
    root_count = math.sqrt(2.0 * total)
    gram_matrix = reduced[:, :vectors] / (2.0 * total)
    symmetric = (gram_matrix + gram_matrix.T) / 2.0
    inverse = inverse_factor(symmetric)
    q_basis = jnp.einsum("kl,alt->akt", inverse, image_rows, precision=lax.Precision.HIGHEST)
    new_basis = jnp.einsum(
        "kl,alt->akt", inverse, basis.astype(jnp.float32), precision=lax.Precision.HIGHEST
    )
    coeffs = jnp.dot(inverse, reduced[:, vectors], precision=lax.Precision.HIGHEST) / root_count
    new_residual = (
        residual
        - jnp.einsum("k,akt->at", coeffs, q_basis, precision=lax.Precision.HIGHEST) / root_count
    )
    return (q_basis, new_basis, coeffs, new_residual)


def solution(mesh):
    in_specs = (
        P(None, None, ("grp", "row")),
        P("grp", "row"),
        P(("row", "grp"), None, None),
        P(None, ("row", "grp")),
        P(),
        P(),
        P(),
    )
    out_specs = (
        P(None, None, ("row", "grp")),
        P(None, None, ("grp", "row")),
        P(),
        P(None, ("row", "grp")),
    )
    return jax.shard_map(local, mesh=mesh, in_specs=in_specs, out_specs=out_specs, check_vma=False)
```

```python
import math

import jax
import jax.numpy as jnp
from jax import lax
from jax.experimental import pallas as pl
from jax.sharding import PartitionSpec as P


def phase_table(freq_index, panel_count):
    wavenumber = (freq_index[0].astype(jnp.float32) + 1.0) * 0.0625
    angles = (jnp.arange(panel_count, dtype=jnp.float32) + 0.5) * 0.5 * wavenumber
    return jnp.stack([jnp.cos(angles), -jnp.sin(angles)]).astype(jnp.bfloat16)


def inverse_factor_kernel(gram_ref, out_ref):
    work = gram_ref[...]
    n = work.shape[0]
    rows = lax.broadcasted_iota(jnp.int32, work.shape, 0)
    cols = lax.broadcasted_iota(jnp.int32, work.shape, 1)
    inverse = (rows == cols).astype(work.dtype)
    for j in range(n):
        scale = lax.rsqrt(work[j:j + 1, j:j + 1])
        column = jnp.where(rows[:, :1] >= j, work[:, j:j + 1] * scale, 0.0)
        row = jnp.where(cols[:1, :] >= j, work[j:j + 1, :] * scale, 0.0)
        work = work - column * row
        lead = inverse[j:j + 1, :] * scale
        inverse = jnp.where(rows == j, lead, inverse - column * lead)
    out_ref[...] = inverse


def inverse_factor(gram):
    return pl.pallas_call(
        inverse_factor_kernel, out_shape=jax.ShapeDtypeStruct(gram.shape, gram.dtype)
    )(gram)


def butterfly_sum(values, axis, count):
    stride = 1
    while stride < count:
        perm = [(i, i ^ stride) for i in range(count)]
        values = values + lax.ppermute(values, axis, perm)
        stride *= 2
    return values


def local(basis, body_infl, wake_columns, residual, te_panels, slot_strip, freq_index):
    n_row = lax.axis_size("row")
    n_grp = lax.axis_size("grp")
    n_dev = n_row * n_grp
    vectors = basis.shape[1]
    stacked_rows = 2 * vectors
    own_cols = basis.shape[2]
    total = own_cols * n_dev
    basis_rows = basis.reshape(stacked_rows, own_cols)
    group_cols = body_infl.shape[0]
    slot_count = slot_strip.shape[0]
    local_slots = wake_columns.shape[0]
    p_size = wake_columns.shape[1]

    row_index = lax.axis_index("row")
    half = n_row // 2
    high = row_index // 2
    parity = row_index % 2
    pieces = [basis_rows]
    for stride in range(2, n_row, 2):
        perm = [(i, i ^ stride) for i in range(n_row)]
        pieces.append(lax.ppermute(basis_rows, "row", perm))
    near = jnp.stack(pieces)[jnp.arange(half, dtype=jnp.int32) ^ high]
    far = lax.ppermute(near, "row", [(i, i ^ 1) for i in range(n_row)])
    blocks = body_infl.reshape(half, 2, own_cols, body_infl.shape[1])
    near_rows = lax.dynamic_index_in_dim(blocks, parity, 1, keepdims=False)
    far_rows = lax.dynamic_index_in_dim(blocks, 1 - parity, 1, keepdims=False)
    near_sums = jnp.einsum("jkp,jpt->kt", near, near_rows, preferred_element_type=jnp.float32)
    near_sums, far = lax.optimization_barrier((near_sums, far))
    partial_sums = near_sums + jnp.einsum(
        "jkp,jpt->kt", far, far_rows, preferred_element_type=jnp.float32
    )

    filled = slot_strip >= 0
    strip_ids = jnp.maximum(slot_strip, 0)
    upper_panel = jnp.where(filled, te_panels[0][strip_ids], -1)
    lower_panel = jnp.where(filled, te_panels[1][strip_ids], -1)
    group_base = lax.axis_index("grp") * group_cols

    def select_for(side):
        first = group_base + (2 * jnp.arange(half, dtype=jnp.int32) + side) * own_cols
        panels = first[:, None] + jnp.arange(own_cols, dtype=jnp.int32)[None, :]
        upper_hits = (panels[:, :, None] == upper_panel).astype(jnp.float32)
        lower_hits = (panels[:, :, None] == lower_panel).astype(jnp.float32)
        return (upper_hits - lower_hits).astype(jnp.bfloat16)

    strength_own = jnp.einsum(
        "jkp,jps->ks", near, select_for(parity), preferred_element_type=jnp.float32
    ) + jnp.einsum("jkp,jps->ks", far, select_for(1 - parity), preferred_element_type=jnp.float32)
    strength_total = strength_own
    for shift in range(1, n_grp):
        perm = [(i, (i + shift) % n_grp) for i in range(n_grp)]
        strength_total = strength_total + lax.ppermute(strength_own, "grp", perm)
    strength = strength_total.astype(jnp.bfloat16)

    phases = phase_table(freq_index, p_size)
    eye = jnp.eye(local_slots, dtype=jnp.bfloat16)
    block_phases = (eye[:, None, :, None] * phases[None, :, None, :]).reshape(
        local_slots * 2, local_slots * p_size
    )
    wake_flat = wake_columns.reshape(local_slots * p_size, total)
    phased = jnp.dot(block_phases, wake_flat, preferred_element_type=jnp.float32)
    phased = phased.astype(jnp.bfloat16).reshape(local_slots * 2, n_dev, own_cols)
    outgoing = phased.transpose(1, 0, 2)
    arrived = lax.all_to_all(outgoing, ("row", "grp"), 0, 0, tiled=True)
    wake_right = arrived.reshape(slot_count * 2, own_cols)

    grp_index = lax.axis_index("grp")
    width = partial_sums.shape[1] // n_grp
    image_part = lax.dynamic_slice_in_dim(partial_sums, grp_index * width, width, axis=1)
    for d in range(1, n_grp):
        block = lax.dynamic_slice_in_dim(partial_sums, (grp_index ^ d) * width, width, axis=1)
        image_part = image_part + lax.ppermute(block, "grp", [(i, i ^ d) for i in range(n_grp)])

    real_part = strength[:vectors]
    imag_part = strength[vectors:]
    top = jnp.stack([real_part, -imag_part], axis=2).reshape(vectors, 2 * slot_count)
    bottom = jnp.stack([imag_part, real_part], axis=2).reshape(vectors, 2 * slot_count)
    wake_left = jnp.concatenate([top, bottom], axis=0)
    wake_part = jnp.dot(wake_left, wake_right, preferred_element_type=jnp.float32)
    image_rows = (image_part + wake_part).reshape(2, vectors, own_cols)

    local_gram = jnp.einsum("akt,alt->kl", image_rows, image_rows, precision=lax.Precision.HIGHEST)
    local_proj = jnp.einsum("akt,at->k", image_rows, residual, precision=lax.Precision.HIGHEST)
    reduced = butterfly_sum(
        butterfly_sum(jnp.concatenate([local_gram, local_proj[:, None]], axis=1), "row", n_row),
        "grp",
        n_grp,
    )
    root_count = math.sqrt(2.0 * total)
    gram_matrix = reduced[:, :vectors] / (2.0 * total)
    symmetric = (gram_matrix + gram_matrix.T) / 2.0
    inverse = inverse_factor(symmetric)
    both = jnp.concatenate([image_rows, basis.astype(jnp.float32)], axis=2)
    solved = jnp.einsum("kl,alt->akt", inverse, both, precision=lax.Precision.HIGHEST)
    q_basis = solved[:, :, :own_cols]
    new_basis = solved[:, :, own_cols:]
    coeffs = jnp.dot(inverse, reduced[:, vectors], precision=lax.Precision.HIGHEST) / root_count
    new_residual = (
        residual
        - jnp.einsum("k,akt->at", coeffs, q_basis, precision=lax.Precision.HIGHEST) / root_count
    )
    return (q_basis, new_basis, coeffs, new_residual)


def solution(mesh):
    in_specs = (
        P(None, None, ("grp", "row")),
        P("grp", "row"),
        P(("row", "grp"), None, None),
        P(None, ("row", "grp")),
        P(),
        P(),
        P(),
    )
    out_specs = (
        P(None, None, ("row", "grp")),
        P(None, None, ("grp", "row")),
        P(),
        P(None, ("row", "grp")),
    )
    return jax.shard_map(local, mesh=mesh, in_specs=in_specs, out_specs=out_specs, check_vma=False)
```

```python
import math

import jax
import jax.numpy as jnp
from jax import lax
from jax.experimental import pallas as pl
from jax.sharding import PartitionSpec as P


def phase_table(freq_index, panel_count):
    wavenumber = (freq_index[0].astype(jnp.float32) + 1.0) * 0.0625
    angles = (jnp.arange(panel_count, dtype=jnp.float32) + 0.5) * 0.5 * wavenumber
    return jnp.stack([jnp.cos(angles), -jnp.sin(angles)]).astype(jnp.bfloat16)


def inverse_factor_kernel(gram_ref, proj_ref, out_ref, coeff_ref):
    work = gram_ref[...]
    n = work.shape[0]
    rows = lax.broadcasted_iota(jnp.int32, work.shape, 0)
    cols = lax.broadcasted_iota(jnp.int32, work.shape, 1)
    inverse = (rows == cols).astype(work.dtype)
    for j in range(n):
        scale = lax.rsqrt(work[j:j + 1, j:j + 1])
        column = jnp.where(rows[:, :1] >= j, work[:, j:j + 1] * scale, 0.0)
        row = jnp.where(cols[:1, :] >= j, work[j:j + 1, :] * scale, 0.0)
        work = work - column * row
        lead = inverse[j:j + 1, :] * scale
        inverse = jnp.where(rows == j, lead, inverse - column * lead)
    out_ref[...] = inverse
    coeff_ref[...] = jnp.sum(inverse * proj_ref[...], axis=1, keepdims=True)


def inverse_factor(gram, proj):
    n = gram.shape[0]
    return pl.pallas_call(
        inverse_factor_kernel,
        out_shape=(
            jax.ShapeDtypeStruct(gram.shape, gram.dtype),
            jax.ShapeDtypeStruct((n, 1), gram.dtype),
        ),
    )(gram, proj.reshape(1, n))


def butterfly_sum(values, axis, count):
    stride = 1
    while stride < count:
        perm = [(i, i ^ stride) for i in range(count)]
        values = values + lax.ppermute(values, axis, perm)
        stride *= 2
    return values


def local(basis, body_infl, wake_columns, residual, te_panels, slot_strip, freq_index):
    n_row = lax.axis_size("row")
    n_grp = lax.axis_size("grp")
    n_dev = n_row * n_grp
    vectors = basis.shape[1]
    stacked_rows = 2 * vectors
    own_cols = basis.shape[2]
    total = own_cols * n_dev
    basis_rows = basis.reshape(stacked_rows, own_cols)
    group_cols = body_infl.shape[0]
    slot_count = slot_strip.shape[0]
    local_slots = wake_columns.shape[0]
    p_size = wake_columns.shape[1]

    row_index = lax.axis_index("row")
    half = n_row // 2
    high = row_index // 2
    parity = row_index % 2
    pieces = [basis_rows]
    for stride in range(2, n_row, 2):
        perm = [(i, i ^ stride) for i in range(n_row)]
        pieces.append(lax.ppermute(basis_rows, "row", perm))
    near = jnp.stack(pieces)[jnp.arange(half, dtype=jnp.int32) ^ high]
    far = lax.ppermute(near, "row", [(i, i ^ 1) for i in range(n_row)])
    blocks = body_infl.reshape(half, 2, own_cols, body_infl.shape[1])
    near_rows = lax.dynamic_index_in_dim(blocks, parity, 1, keepdims=False)
    far_rows = lax.dynamic_index_in_dim(blocks, 1 - parity, 1, keepdims=False)
    near_sums = jnp.einsum("jkp,jpt->kt", near, near_rows, preferred_element_type=jnp.float32)
    near_sums, far = lax.optimization_barrier((near_sums, far))
    partial_sums = near_sums + jnp.einsum(
        "jkp,jpt->kt", far, far_rows, preferred_element_type=jnp.float32
    )

    filled = slot_strip >= 0
    strip_ids = jnp.maximum(slot_strip, 0)
    upper_panel = jnp.where(filled, te_panels[0][strip_ids], -1)
    lower_panel = jnp.where(filled, te_panels[1][strip_ids], -1)
    group_base = lax.axis_index("grp") * group_cols

    def select_for(side):
        first = group_base + (2 * jnp.arange(half, dtype=jnp.int32) + side) * own_cols
        panels = first[:, None] + jnp.arange(own_cols, dtype=jnp.int32)[None, :]
        upper_hits = (panels[:, :, None] == upper_panel).astype(jnp.float32)
        lower_hits = (panels[:, :, None] == lower_panel).astype(jnp.float32)
        return (upper_hits - lower_hits).astype(jnp.bfloat16)

    strength_own = jnp.einsum(
        "jkp,jps->ks", near, select_for(parity), preferred_element_type=jnp.float32
    ) + jnp.einsum("jkp,jps->ks", far, select_for(1 - parity), preferred_element_type=jnp.float32)
    strength_total = strength_own
    for shift in range(1, n_grp):
        perm = [(i, (i + shift) % n_grp) for i in range(n_grp)]
        strength_total = strength_total + lax.ppermute(strength_own, "grp", perm)
    strength = strength_total.astype(jnp.bfloat16)

    phases = phase_table(freq_index, p_size)
    eye = jnp.eye(local_slots, dtype=jnp.bfloat16)
    block_phases = (eye[:, None, :, None] * phases[None, :, None, :]).reshape(
        local_slots * 2, local_slots * p_size
    )
    wake_flat = wake_columns.reshape(local_slots * p_size, total)
    phased = jnp.dot(block_phases, wake_flat, preferred_element_type=jnp.float32)
    phased = phased.astype(jnp.bfloat16).reshape(local_slots * 2, n_dev, own_cols)
    outgoing = phased.transpose(1, 0, 2)
    arrived = lax.all_to_all(outgoing, ("row", "grp"), 0, 0, tiled=True)
    wake_right = arrived.reshape(slot_count * 2, own_cols)

    grp_index = lax.axis_index("grp")
    width = partial_sums.shape[1] // n_grp
    image_part = lax.dynamic_slice_in_dim(partial_sums, grp_index * width, width, axis=1)
    for d in range(1, n_grp):
        block = lax.dynamic_slice_in_dim(partial_sums, (grp_index ^ d) * width, width, axis=1)
        image_part = image_part + lax.ppermute(block, "grp", [(i, i ^ d) for i in range(n_grp)])

    real_part = strength[:vectors]
    imag_part = strength[vectors:]
    top = jnp.stack([real_part, -imag_part], axis=2).reshape(vectors, 2 * slot_count)
    bottom = jnp.stack([imag_part, real_part], axis=2).reshape(vectors, 2 * slot_count)
    wake_left = jnp.concatenate([top, bottom], axis=0)
    wake_part = jnp.dot(wake_left, wake_right, preferred_element_type=jnp.float32)
    image_rows = (image_part + wake_part).reshape(2, vectors, own_cols)

    local_gram = jnp.einsum("akt,alt->kl", image_rows, image_rows, precision=lax.Precision.HIGHEST)
    local_proj = jnp.einsum("akt,at->k", image_rows, residual, precision=lax.Precision.HIGHEST)
    reduced = butterfly_sum(
        butterfly_sum(jnp.concatenate([local_gram, local_proj[:, None]], axis=1), "row", n_row),
        "grp",
        n_grp,
    )
    root_count = math.sqrt(2.0 * total)
    gram_matrix = reduced[:, :vectors] / (2.0 * total)
    symmetric = (gram_matrix + gram_matrix.T) / 2.0
    inverse, mapped = inverse_factor(symmetric, reduced[:, vectors])
    both = jnp.concatenate([image_rows, basis.astype(jnp.float32)], axis=2)
    solved = jnp.einsum("kl,alt->akt", inverse, both, precision=lax.Precision.HIGHEST)
    q_basis = solved[:, :, :own_cols]
    new_basis = solved[:, :, own_cols:]
    coeffs = mapped[:, 0] / root_count
    new_residual = (
        residual
        - jnp.einsum("k,akt->at", coeffs, q_basis, precision=lax.Precision.HIGHEST) / root_count
    )
    return (q_basis, new_basis, coeffs, new_residual)


def solution(mesh):
    in_specs = (
        P(None, None, ("grp", "row")),
        P("grp", "row"),
        P(("row", "grp"), None, None),
        P(None, ("row", "grp")),
        P(),
        P(),
        P(),
    )
    out_specs = (
        P(None, None, ("row", "grp")),
        P(None, None, ("grp", "row")),
        P(),
        P(None, ("row", "grp")),
    )
    return jax.shard_map(local, mesh=mesh, in_specs=in_specs, out_specs=out_specs, check_vma=False)
```

```python
import math

import jax
import jax.numpy as jnp
from jax import lax
from jax.experimental import pallas as pl
from jax.sharding import PartitionSpec as P


def phase_table(freq_index, panel_count):
    wavenumber = (freq_index[0].astype(jnp.float32) + 1.0) * 0.0625
    angles = (jnp.arange(panel_count, dtype=jnp.float32) + 0.5) * 0.5 * wavenumber
    return jnp.stack([jnp.cos(angles), -jnp.sin(angles)]).astype(jnp.bfloat16)


def inverse_factor_kernel(gram_ref, proj_ref, out_ref, coeff_ref):
    work = gram_ref[...]
    n = work.shape[0]
    rows = lax.broadcasted_iota(jnp.int32, work.shape, 0)
    cols = lax.broadcasted_iota(jnp.int32, work.shape, 1)
    inverse = (rows == cols).astype(work.dtype)
    for j in range(n):
        scale = lax.rsqrt(work[j:j + 1, j:j + 1])
        column = jnp.where(rows[:, :1] >= j, work[:, j:j + 1] * scale, 0.0)
        row = jnp.where(cols[:1, :] >= j, work[j:j + 1, :] * scale, 0.0)
        work = work - column * row
        lead = inverse[j:j + 1, :] * scale
        inverse = jnp.where(rows == j, lead, inverse - column * lead)
    out_ref[...] = inverse
    coeff_ref[...] = jnp.sum(inverse * proj_ref[...], axis=1, keepdims=True)


def inverse_factor(gram, proj):
    n = gram.shape[0]
    return pl.pallas_call(
        inverse_factor_kernel,
        out_shape=(
            jax.ShapeDtypeStruct(gram.shape, gram.dtype),
            jax.ShapeDtypeStruct((n, 1), gram.dtype),
        ),
    )(gram, proj.reshape(1, n))


def butterfly_sum(values, axis, count):
    stride = 1
    while stride < count:
        perm = [(i, i ^ stride) for i in range(count)]
        values = values + lax.ppermute(values, axis, perm)
        stride *= 2
    return values


def local(basis, body_infl, wake_columns, residual, te_panels, slot_strip, freq_index):
    n_row = lax.axis_size("row")
    n_grp = lax.axis_size("grp")
    n_dev = n_row * n_grp
    vectors = basis.shape[1]
    stacked_rows = 2 * vectors
    own_cols = basis.shape[2]
    total = own_cols * n_dev
    basis_rows = basis.reshape(stacked_rows, own_cols)
    group_cols = body_infl.shape[0]
    slot_count = slot_strip.shape[0]
    local_slots = wake_columns.shape[0]
    p_size = wake_columns.shape[1]

    row_index = lax.axis_index("row")
    half = n_row // 2
    high = row_index // 2
    parity = row_index % 2
    pieces = [basis_rows]
    for stride in range(2, n_row, 2):
        perm = [(i, i ^ stride) for i in range(n_row)]
        pieces.append(lax.ppermute(basis_rows, "row", perm))
    near = jnp.stack(pieces)[jnp.arange(half, dtype=jnp.int32) ^ high]
    far = lax.ppermute(near, "row", [(i, i ^ 1) for i in range(n_row)])
    blocks = body_infl.reshape(half, 2, own_cols, body_infl.shape[1])
    near_rows = lax.dynamic_index_in_dim(blocks, parity, 1, keepdims=False)
    far_rows = lax.dynamic_index_in_dim(blocks, 1 - parity, 1, keepdims=False)
    near_sums = jnp.einsum("jkp,jpt->kt", near, near_rows, preferred_element_type=jnp.float32)
    near_sums, far = lax.optimization_barrier((near_sums, far))
    partial_sums = near_sums + jnp.einsum(
        "jkp,jpt->kt", far, far_rows, preferred_element_type=jnp.float32
    )

    filled = slot_strip >= 0
    strip_ids = jnp.maximum(slot_strip, 0)
    upper_panel = jnp.where(filled, te_panels[0][strip_ids], -1)
    lower_panel = jnp.where(filled, te_panels[1][strip_ids], -1)
    group_base = lax.axis_index("grp") * group_cols

    def select_for(side):
        first = group_base + (2 * jnp.arange(half, dtype=jnp.int32) + side) * own_cols
        panels = first[:, None] + jnp.arange(own_cols, dtype=jnp.int32)[None, :]
        upper_hits = (panels[:, :, None] == upper_panel).astype(jnp.float32)
        lower_hits = (panels[:, :, None] == lower_panel).astype(jnp.float32)
        return (upper_hits - lower_hits).astype(jnp.bfloat16)

    strength_own = jnp.einsum(
        "jkp,jps->ks", near, select_for(parity), preferred_element_type=jnp.float32
    ) + jnp.einsum("jkp,jps->ks", far, select_for(1 - parity), preferred_element_type=jnp.float32)
    strength_total = strength_own
    for shift in range(1, n_grp):
        perm = [(i, (i + shift) % n_grp) for i in range(n_grp)]
        strength_total = strength_total + lax.ppermute(strength_own, "grp", perm)
    strength = strength_total.astype(jnp.bfloat16)

    phases = phase_table(freq_index, p_size)
    eye = jnp.eye(local_slots, dtype=jnp.bfloat16)
    block_phases = (eye[:, None, :, None] * phases[None, :, None, :]).reshape(
        local_slots * 2, local_slots * p_size
    )
    wake_flat = wake_columns.reshape(local_slots * p_size, total)
    phased = jnp.dot(block_phases, wake_flat, preferred_element_type=jnp.float32)
    phased = phased.astype(jnp.bfloat16).reshape(local_slots * 2, n_dev, own_cols)
    outgoing = phased.transpose(1, 0, 2)
    arrived = lax.all_to_all(outgoing, ("row", "grp"), 0, 0, tiled=True)
    wake_right = arrived.reshape(slot_count * 2, own_cols)

    grp_index = lax.axis_index("grp")
    width = partial_sums.shape[1] // n_grp
    image_part = lax.dynamic_slice_in_dim(partial_sums, grp_index * width, width, axis=1)
    for d in range(1, n_grp):
        block = lax.dynamic_slice_in_dim(partial_sums, (grp_index ^ d) * width, width, axis=1)
        image_part = image_part + lax.ppermute(block, "grp", [(i, i ^ d) for i in range(n_grp)])

    real_part = strength[:vectors]
    imag_part = strength[vectors:]
    top = jnp.stack([real_part, -imag_part], axis=2).reshape(vectors, 2 * slot_count)
    bottom = jnp.stack([imag_part, real_part], axis=2).reshape(vectors, 2 * slot_count)
    wake_left = jnp.concatenate([top, bottom], axis=0)
    wake_part = jnp.dot(wake_left, wake_right, preferred_element_type=jnp.float32)
    image_rows = (image_part + wake_part).reshape(2, vectors, own_cols)

    local_gram = jnp.einsum("akt,alt->kl", image_rows, image_rows, precision=lax.Precision.HIGHEST)
    local_proj = jnp.einsum("akt,at->k", image_rows, residual, precision=lax.Precision.HIGHEST)
    reduced = butterfly_sum(
        butterfly_sum(jnp.concatenate([local_gram, local_proj[:, None]], axis=1), "row", n_row),
        "grp",
        n_grp,
    )
    root_count = math.sqrt(2.0 * total)
    gram_matrix = reduced[:, :vectors] / (2.0 * total)
    symmetric = (gram_matrix + gram_matrix.T) / 2.0
    inverse, mapped = inverse_factor(symmetric, reduced[:, vectors])
    q_basis = jnp.einsum("kl,alt->akt", inverse, image_rows, precision=lax.Precision.HIGHEST)
    new_basis = jnp.einsum(
        "kl,alt->akt", inverse, basis.astype(jnp.float32), precision=lax.Precision.HIGHEST
    )
    coeffs = mapped[:, 0] / root_count
    new_residual = (
        residual
        - jnp.einsum("k,akt->at", coeffs, q_basis, precision=lax.Precision.HIGHEST) / root_count
    )
    return (q_basis, new_basis, coeffs, new_residual)


def solution(mesh):
    in_specs = (
        P(None, None, ("grp", "row")),
        P("grp", "row"),
        P(("row", "grp"), None, None),
        P(None, ("row", "grp")),
        P(),
        P(),
        P(),
    )
    out_specs = (
        P(None, None, ("row", "grp")),
        P(None, None, ("grp", "row")),
        P(),
        P(None, ("row", "grp")),
    )
    return jax.shard_map(local, mesh=mesh, in_specs=in_specs, out_specs=out_specs, check_vma=False)
```

```python
import math

import jax
import jax.numpy as jnp
from jax import lax
from jax.experimental import pallas as pl
from jax.sharding import PartitionSpec as P


def phase_table(freq_index, panel_count):
    wavenumber = (freq_index[0].astype(jnp.float32) + 1.0) * 0.0625
    angles = (jnp.arange(panel_count, dtype=jnp.float32) + 0.5) * 0.5 * wavenumber
    return jnp.stack([jnp.cos(angles), -jnp.sin(angles)]).astype(jnp.bfloat16)


def inverse_factor_kernel(gram_ref, proj_ref, out_ref, coeff_ref):
    work = gram_ref[...]
    n = work.shape[0]
    rows = lax.broadcasted_iota(jnp.int32, work.shape, 0)
    cols = lax.broadcasted_iota(jnp.int32, work.shape, 1)
    inverse = (rows == cols).astype(work.dtype)
    for j in range(n):
        scale = lax.rsqrt(work[j:j + 1, j:j + 1])
        column = jnp.where(rows[:, :1] >= j, work[:, j:j + 1] * scale, 0.0)
        row = jnp.where(cols[:1, :] >= j, work[j:j + 1, :] * scale, 0.0)
        work = work - column * row
        lead = inverse[j:j + 1, :] * scale
        inverse = jnp.where(rows == j, lead, inverse - column * lead)
    out_ref[...] = inverse
    coeff_ref[...] = jnp.sum(inverse * proj_ref[...], axis=1, keepdims=True)


def inverse_factor(gram, proj):
    n = gram.shape[0]
    return pl.pallas_call(
        inverse_factor_kernel,
        out_shape=(
            jax.ShapeDtypeStruct(gram.shape, gram.dtype),
            jax.ShapeDtypeStruct((n, 1), gram.dtype),
        ),
    )(gram, proj.reshape(1, n))


def butterfly_sum(values, axis, count):
    stride = 1
    while stride < count:
        perm = [(i, i ^ stride) for i in range(count)]
        values = values + lax.ppermute(values, axis, perm)
        stride *= 2
    return values


def local(basis, body_infl, wake_columns, residual, te_panels, slot_strip, freq_index):
    n_row = lax.axis_size("row")
    n_grp = lax.axis_size("grp")
    n_dev = n_row * n_grp
    vectors = basis.shape[1]
    stacked_rows = 2 * vectors
    own_cols = basis.shape[2]
    total = own_cols * n_dev
    basis_rows = basis.reshape(stacked_rows, own_cols)
    group_cols = body_infl.shape[0]
    slot_count = slot_strip.shape[0]
    local_slots = wake_columns.shape[0]
    p_size = wake_columns.shape[1]

    row_index = lax.axis_index("row")
    half = n_row // 2
    high = row_index // 2
    parity = row_index % 2
    pieces = [basis_rows]
    for stride in range(2, n_row, 2):
        perm = [(i, i ^ stride) for i in range(n_row)]
        pieces.append(lax.ppermute(basis_rows, "row", perm))
    near = jnp.stack(pieces)[jnp.arange(half, dtype=jnp.int32) ^ high]
    far = lax.ppermute(near, "row", [(i, i ^ 1) for i in range(n_row)])
    blocks = body_infl.reshape(half, 2, own_cols, body_infl.shape[1])
    near_rows = lax.dynamic_index_in_dim(blocks, parity, 1, keepdims=False)
    far_rows = lax.dynamic_index_in_dim(blocks, 1 - parity, 1, keepdims=False)
    near_sums = jnp.einsum("jkp,jpt->kt", near, near_rows, preferred_element_type=jnp.float32)
    near_sums, far = lax.optimization_barrier((near_sums, far))
    partial_sums = near_sums + jnp.einsum(
        "jkp,jpt->kt", far, far_rows, preferred_element_type=jnp.float32
    )

    filled = slot_strip >= 0
    strip_ids = jnp.maximum(slot_strip, 0)
    upper_panel = jnp.where(filled, te_panels[0][strip_ids], -1)
    lower_panel = jnp.where(filled, te_panels[1][strip_ids], -1)
    group_base = lax.axis_index("grp") * group_cols

    def select_for(side):
        first = group_base + (2 * jnp.arange(half, dtype=jnp.int32) + side) * own_cols
        panels = first[:, None] + jnp.arange(own_cols, dtype=jnp.int32)[None, :]
        upper_hits = (panels[:, :, None] == upper_panel).astype(jnp.float32)
        lower_hits = (panels[:, :, None] == lower_panel).astype(jnp.float32)
        return (upper_hits - lower_hits).astype(jnp.bfloat16)

    strength_own = jnp.einsum(
        "jkp,jps->ks", near, select_for(parity), preferred_element_type=jnp.float32
    ) + jnp.einsum("jkp,jps->ks", far, select_for(1 - parity), preferred_element_type=jnp.float32)
    strength = butterfly_sum(strength_own, "grp", n_grp).astype(jnp.bfloat16)

    phases = phase_table(freq_index, p_size)
    eye = jnp.eye(local_slots, dtype=jnp.bfloat16)
    block_phases = (eye[:, None, :, None] * phases[None, :, None, :]).reshape(
        local_slots * 2, local_slots * p_size
    )
    wake_flat = wake_columns.reshape(local_slots * p_size, total)
    phased = jnp.dot(block_phases, wake_flat, preferred_element_type=jnp.float32)
    phased = phased.astype(jnp.bfloat16).reshape(local_slots * 2, n_dev, own_cols)
    outgoing = phased.transpose(1, 0, 2)
    arrived = lax.all_to_all(outgoing, ("row", "grp"), 0, 0, tiled=True)
    wake_right = arrived.reshape(slot_count * 2, own_cols)

    grp_index = lax.axis_index("grp")
    width = partial_sums.shape[1] // n_grp
    image_part = lax.dynamic_slice_in_dim(partial_sums, grp_index * width, width, axis=1)
    for d in range(1, n_grp):
        block = lax.dynamic_slice_in_dim(partial_sums, (grp_index ^ d) * width, width, axis=1)
        image_part = image_part + lax.ppermute(block, "grp", [(i, i ^ d) for i in range(n_grp)])

    real_part = strength[:vectors]
    imag_part = strength[vectors:]
    top = jnp.stack([real_part, -imag_part], axis=2).reshape(vectors, 2 * slot_count)
    bottom = jnp.stack([imag_part, real_part], axis=2).reshape(vectors, 2 * slot_count)
    wake_left = jnp.concatenate([top, bottom], axis=0)
    wake_part = jnp.dot(wake_left, wake_right, preferred_element_type=jnp.float32)
    image_rows = (image_part + wake_part).reshape(2, vectors, own_cols)

    local_gram = jnp.einsum("akt,alt->kl", image_rows, image_rows, precision=lax.Precision.HIGHEST)
    local_proj = jnp.einsum("akt,at->k", image_rows, residual, precision=lax.Precision.HIGHEST)
    reduced = butterfly_sum(
        butterfly_sum(jnp.concatenate([local_gram, local_proj[:, None]], axis=1), "row", n_row),
        "grp",
        n_grp,
    )
    root_count = math.sqrt(2.0 * total)
    gram_matrix = reduced[:, :vectors] / (2.0 * total)
    symmetric = (gram_matrix + gram_matrix.T) / 2.0
    inverse, mapped = inverse_factor(symmetric, reduced[:, vectors])
    q_basis = jnp.einsum("kl,alt->akt", inverse, image_rows, precision=lax.Precision.HIGHEST)
    new_basis = jnp.einsum(
        "kl,alt->akt", inverse, basis.astype(jnp.float32), precision=lax.Precision.HIGHEST
    )
    coeffs = mapped[:, 0] / root_count
    new_residual = (
        residual
        - jnp.einsum("k,akt->at", coeffs, q_basis, precision=lax.Precision.HIGHEST) / root_count
    )
    return (q_basis, new_basis, coeffs, new_residual)


def solution(mesh):
    in_specs = (
        P(None, None, ("grp", "row")),
        P("grp", "row"),
        P(("row", "grp"), None, None),
        P(None, ("row", "grp")),
        P(),
        P(),
        P(),
    )
    out_specs = (
        P(None, None, ("row", "grp")),
        P(None, None, ("grp", "row")),
        P(),
        P(None, ("row", "grp")),
    )
    return jax.shard_map(local, mesh=mesh, in_specs=in_specs, out_specs=out_specs, check_vma=False)
```
